1024 devices in a mesh: task: 8 (over y), fsdp: 128 (over z, x, core).
Axes of the slice: x: 4, y: 8, z: 16, core: 2. Of those that a mesh axis runs over, the one named last changes fastest.
Arguments:
- contexts: bfloat16 [8, 24576, 4096], P('task', 'fsdp'), may hold values from -3400 to 3400
- cotangents: bfloat16 [8, 24576, 4096], P('task', 'fsdp'), may hold values from -3400 to 3400
- adapter: bfloat16 [4096, 256], P('fsdp'), may hold values from -0.09375 to 0.09375
- moment_one: float32 [4096, 256], P('fsdp', 'task'), may hold values from -6 to 6
- moment_two: float32 [4096, 256], P('fsdp', 'task'), may hold values from 0.01 to 10
Outputs:
- first_moment: float32 [4096, 256], P('fsdp', 'task')
- second_moment: float32 [4096, 256], P('fsdp', 'task')
- adam_step: float32 [4096, 256], P('fsdp', 'task')
The draws below stay inside these ranges and needn't reach their ends.
All inputs are finite; a program needn't handle non-finite values.
Results may differ from the reference program's by a relative error of at most 0.0004.
The reference program's roundings to bfloat16 on the way (of `low` and `back`) count: a program that leaves them out, or rounds other values in their place, can miss the bound.
Values may be sent and summed in bfloat16 or wider, within the bound.
No kernel may reach another device: no remote copies, remote signals or barrier semaphores. Data moves between devices by JAX's collectives and lax.ppermute only.
A program may use at most 32 MiB of HBM per device.

```python
import math
import jax
import jax.numpy as jnp
from jax import lax

D = 4096
INNER = 4096
RANK = 128
TOKENS = 24576
TASKS = 8


def scaled_field(key, width):
    keys = jax.random.split(key, 4)
    ramp = jnp.arange(width, dtype=jnp.float32) / float(width - 1)
    feature_scale = jnp.exp(math.log(10.0) * ramp) * jax.random.uniform(keys[0], (width,), jnp.float32, 0.7, 1.4)
    token_scale = jnp.exp(jax.random.uniform(keys[1], (TASKS, TOKENS, 1), jnp.float32, 0.0, math.log(10.0)))
    task_scale = jnp.exp(jax.random.uniform(keys[2], (TASKS, 1, 1), jnp.float32, 0.0, math.log(4.0)))
    noise = jax.random.truncated_normal(keys[3], -6.0, 6.0, (TASKS, TOKENS, width), jnp.float32)
    return (noise * token_scale * task_scale * feature_scale).astype(jnp.bfloat16)


def draw_contexts(key, part):
    return scaled_field(jax.random.fold_in(key, 11), INNER)


def draw_cotangents(key, part):
    return scaled_field(jax.random.fold_in(key, 23), D)


def levels(key, shape, cuts, low, top_value):
    def one(dim, parts):
        heights = jax.random.uniform(jax.random.fold_in(jax.random.fold_in(key, 6), dim), (parts,), jnp.float32, low / len(cuts), top_value / len(cuts))
        return jnp.repeat(jnp.exp(heights), shape[dim] // parts).reshape((-1,) + (1,) * (len(shape) - dim - 1))

    level = one(*cuts[0])
    for cut in cuts[1:]:
        level = level * one(*cut)
    return level


def bell_draw(stream_key, shape, deviation, bound, pieces=(), kind=jnp.bfloat16):
    array = deviation * jax.random.normal(stream_key, shape, jnp.float32)
    if pieces:
        array = array * levels(stream_key, shape, pieces, -0.22, 0.18)
    return jnp.clip(array, -bound, bound).astype(kind)


def setup_inputs(seed: int = 0) -> dict:
    key_list = jax.random.split(jax.random.key(seed), 6)
    contexts = draw_contexts(jax.random.fold_in(key_list[5], 71), 0)
    cotangents = draw_cotangents(jax.random.fold_in(key_list[5], 71), 0)
    adapter = bell_draw(key_list[2], (D, 2 * RANK), D ** -0.5, 0.09375, ((0, 128),))
    moment_one = bell_draw(key_list[3], (D, 2 * RANK), 1.0, 6.0, ((0, 128), (1, 8)), jnp.float32)
    moment_two = jnp.clip(jnp.exp(math.log(10.0) - 6.9077553 * jax.random.uniform(key_list[4], (D, 2 * RANK), jnp.float32) ** levels(key_list[4], (D, 2 * RANK), ((0, 128), (1, 8)), -0.2, 0.2)), 0.01, 10.0)
    return {"contexts": contexts, "cotangents": cotangents, "adapter": adapter, "moment_one": moment_one, "moment_two": moment_two}


def eliminate(matrix, vector):
    extent = vector.shape[0]
    matrix_rows = [matrix[position] for position in range(extent)]
    values = [vector[position] for position in range(extent)]
    for column in range(extent):
        for target in range(column + 1, extent):
            factor = matrix_rows[target][column] / matrix_rows[column][column]
            matrix_rows[target] = matrix_rows[target] - factor * matrix_rows[column]
            values[target] = values[target] - factor * values[column]
    answer = [values[0] for position in range(extent)]
    for column in reversed(range(extent)):
        running = values[column]
        for follow in range(column + 1, extent):
            running = running - matrix_rows[column][follow] * answer[follow]
        answer[column] = running / matrix_rows[column][column]
    return jnp.stack(answer)

def task_weights(gram_matrix):
    task_norms = jnp.sqrt(jnp.diagonal(gram_matrix))
    right_side = gram_matrix[0, 0] / task_norms[0] - gram_matrix[0, 1:] / task_norms[1:]
    system = (gram_matrix[0, 0] - gram_matrix[1:, 0])[:, None] / task_norms[0] - (gram_matrix[0, 1:][None, :] - gram_matrix[1:, 1:]) / task_norms[1:][None, :]
    solution = eliminate(system.T, right_side)
    return jnp.concatenate([jnp.reshape(1.0 - jnp.sum(solution), (1,)), solution])

def adam_update(combined, grad_norm, moment_one, moment_two):
    clipped = combined * (math.sqrt(2 * RANK * D) / grad_norm)
    first_moment = 0.9 * moment_one + 0.1 * clipped
    second_moment = 0.95 * moment_two + 0.05 * clipped * clipped
    adam_step = first_moment / (1.0 - 0.9 ** 20) / (jnp.sqrt(second_moment / (1.0 - 0.95 ** 20)) + 1e-08)
    return (first_moment, second_moment, adam_step)

def reference(contexts, cotangents, adapter, moment_one, moment_two):

    def one_task(tensor_pair):
        context_rows, cotangent_rows = tensor_pair
        low = jnp.dot(context_rows, adapter[:, :RANK], preferred_element_type=jnp.float32).astype(adapter.dtype)
        back = jnp.dot(cotangent_rows, adapter[:, RANK:], preferred_element_type=jnp.float32).astype(adapter.dtype)
        down_grad = jnp.dot(context_rows.T, back, preferred_element_type=jnp.float32)
        up_grad = jnp.dot(cotangent_rows.T, low, preferred_element_type=jnp.float32)
        return jnp.concatenate([down_grad, up_grad], axis=1)
    grads = lax.map(one_task, (contexts, cotangents))
    gram_matrix = jnp.einsum('sij,tij->st', grads, grads, precision=lax.Precision.HIGHEST)
    task_alpha = task_weights(gram_matrix)
    combined = jnp.einsum('t,tij->ij', task_alpha, grads, precision=lax.Precision.HIGHEST)
    grad_norm = jnp.sqrt(1e-06 + jnp.sum(combined * combined))
    first_moment, second_moment, adam_step = adam_update(combined, grad_norm, moment_one, moment_two)
    return (first_moment, second_moment, adam_step)
```

```python
import math

import jax
import jax.numpy as jnp
from jax import lax
from jax.sharding import Mesh
from jax.sharding import PartitionSpec as P

D = 4096
RANK = 128
FSDP = ("z", "x", "core")
ALL_AXES = ("core", "x", "z", "task")


def eliminate(matrix, vector):
    extent = vector.shape[0]
    matrix_rows = [matrix[position] for position in range(extent)]
    values = [vector[position] for position in range(extent)]
    for column in range(extent):
        for target in range(column + 1, extent):
            factor = matrix_rows[target][column] / matrix_rows[column][column]
            matrix_rows[target] = matrix_rows[target] - factor * matrix_rows[column]
            values[target] = values[target] - factor * values[column]
    answer = [values[0] for position in range(extent)]
    for column in reversed(range(extent)):
        running = values[column]
        for follow in range(column + 1, extent):
            running = running - matrix_rows[column][follow] * answer[follow]
        answer[column] = running / matrix_rows[column][column]
    return jnp.stack(answer)


def task_weights(gram_matrix):
    task_norms = jnp.sqrt(jnp.diagonal(gram_matrix))
    right_side = gram_matrix[0, 0] / task_norms[0] - gram_matrix[0, 1:] / task_norms[1:]
    system = (gram_matrix[0, 0] - gram_matrix[1:, 0])[:, None] / task_norms[0] - (
        gram_matrix[0, 1:][None, :] - gram_matrix[1:, 1:]
    ) / task_norms[1:][None, :]
    solution = eliminate(system.T, right_side)
    return jnp.concatenate([jnp.reshape(1.0 - jnp.sum(solution), (1,)), solution])


def butterfly_sum(value, axis):
    size = lax.axis_size(axis)
    step = 1
    while step < size:
        pairs = [(i, i ^ step) for i in range(size)]
        value = value + lax.ppermute(value, axis, pairs)
        step *= 2
    return value


def body(contexts, cotangents, adapter, moment_one, moment_two):
    own_context = contexts[0]
    own_cotangent = cotangents[0]
    rank_width = adapter.shape[1] // 2
    piece = adapter
    for axis in ("core", "x", "z"):
        piece = lax.all_gather(piece, axis, axis=0, tiled=True)
    low = jnp.dot(own_context, piece[:, :rank_width], preferred_element_type=jnp.float32).astype(jnp.bfloat16)
    back = jnp.dot(own_cotangent, piece[:, rank_width:], preferred_element_type=jnp.float32).astype(jnp.bfloat16)
    down_part = lax.dot_general(
        own_context, back, (((0,), (0,)), ((), ())), preferred_element_type=jnp.float32
    )
    up_part = lax.dot_general(
        own_cotangent, low, (((0,), (0,)), ((), ())), preferred_element_type=jnp.float32
    )
    grad_rows = jnp.concatenate([down_part, up_part], axis=1)
    for axis in ("z", "x", "core"):
        grad_rows = lax.psum_scatter(grad_rows, axis, scatter_dimension=0, tiled=True)
    tasks = lax.axis_size("task")
    rows, width = grad_rows.shape
    blocks = grad_rows.reshape(rows, tasks, width // tasks).transpose(1, 0, 2)
    pieces = lax.all_to_all(blocks, "task", 0, 0, tiled=True)
    partial_gram = jnp.einsum("sij,tij->st", pieces, pieces, precision=lax.Precision.HIGHEST)
    gram_matrix = partial_gram
    for axis in ALL_AXES:
        gram_matrix = butterfly_sum(gram_matrix, axis)
    task_alpha = task_weights(gram_matrix)
    combined = jnp.einsum("t,tij->ij", task_alpha, pieces, precision=lax.Precision.HIGHEST)
    squared = jnp.dot(
        task_alpha, jnp.dot(gram_matrix, task_alpha, precision=lax.Precision.HIGHEST),
        precision=lax.Precision.HIGHEST,
    )
    grad_norm = jnp.sqrt(1e-06 + squared)
    clipped = combined * (math.sqrt(2 * RANK * D) / grad_norm)
    first_moment = 0.9 * moment_one + 0.1 * clipped
    second_moment = 0.95 * moment_two + 0.05 * clipped * clipped
    adam_step = (
        first_moment / (1.0 - 0.9**20) / (jnp.sqrt(second_moment / (1.0 - 0.95**20)) + 1e-08)
    )
    return (first_moment, second_moment, adam_step)


def solution(mesh):
    tasks, fsdp = mesh.devices.shape
    split = Mesh(mesh.devices.reshape(tasks, fsdp // 8, 4, 2), ("task",) + FSDP)
    in_specs = (
        P("task", FSDP, None),
        P("task", FSDP, None),
        P(FSDP, None),
        P(FSDP, "task"),
        P(FSDP, "task"),
    )
    out_specs = (P(FSDP, "task"), P(FSDP, "task"), P(FSDP, "task"))
    return jax.shard_map(body, mesh=split, in_specs=in_specs, out_specs=out_specs, check_vma=False)
```

```python
import math

import jax
import jax.numpy as jnp
from jax import lax
from jax.experimental import pallas as pl
from jax.sharding import Mesh
from jax.sharding import PartitionSpec as P

D = 4096
RANK = 128
FSDP = ("z", "x", "core")
ALL_AXES = ("core", "x", "z", "task")


def tail_kernel(gram_ref, gramt_ref, pieces_ref, m1_ref, m2_ref, first_ref, second_ref, step_ref):
    gram = gram_ref[...]
    kt = gramt_ref[...]
    shape = gram.shape
    row = lax.broadcasted_iota(jnp.int32, shape, 0)
    lane = lax.broadcasted_iota(jnp.int32, shape, 1)

    def lanes(x):
        return jnp.sum(x, axis=1, keepdims=True)

    def sublanes(x):
        return jnp.sum(x, axis=0, keepdims=True)

    def pick(x, r, l):
        return lanes(sublanes(jnp.where((row == r) & (lane == l), x, 0.0)))

    norm_col = jnp.sqrt(lanes(jnp.where(row == lane, gram, 0.0)))
    k00 = pick(gram, 0, 0)
    n0 = jnp.sqrt(k00)
    k_i0 = sublanes(jnp.where(row == 0, kt, 0.0))
    k_0j = lanes(jnp.where(lane == 0, kt, 0.0))
    system = (k00 - k_i0) / n0 - (k_0j - kt) / norm_col
    right = k00 / n0 - k_0j / norm_col
    aug = jnp.where(lane == 0, right, system)
    tasks = pieces_ref.shape[0]
    for column in range(1, tasks):
        pivot_row = sublanes(jnp.where(row == column, aug, 0.0))
        column_vals = lanes(jnp.where(lane == column, aug, 0.0))
        pivot = lanes(jnp.where(lane[:1] == column, pivot_row, 0.0))
        factor = column_vals / pivot
        aug = jnp.where(row > column, aug - factor * pivot_row, aug)
    answer = [None] * tasks
    lane_row = lax.broadcasted_iota(jnp.int32, (1, shape[1]), 1)
    row_col = lax.broadcasted_iota(jnp.int32, (shape[0], 1), 0)
    for column in reversed(range(1, tasks)):
        pivot_row = sublanes(jnp.where(row == column, aug, 0.0))
        running = lanes(jnp.where(lane_row == 0, pivot_row, 0.0))
        for follow in range(column + 1, tasks):
            running = running - lanes(jnp.where(lane_row == follow, pivot_row, 0.0)) * answer[follow]
        answer[column] = running / lanes(jnp.where(lane_row == column, pivot_row, 0.0))
    total = answer[1]
    for column in range(2, tasks):
        total = total + answer[column]
    answer[0] = 1.0 - total
    alpha_row = jnp.zeros((1, shape[1]), jnp.float32)
    alpha_col = jnp.zeros((shape[0], 1), jnp.float32)
    for t in range(tasks):
        alpha_row = jnp.where(lane_row == t, answer[t], alpha_row)
        alpha_col = jnp.where(row_col == t, answer[t], alpha_col)
    combined = answer[0] * pieces_ref[0]
    for t in range(1, tasks):
        combined = combined + answer[t] * pieces_ref[t]
    squared = sublanes(alpha_col * lanes(gram * alpha_row))
    grad_norm = jnp.sqrt(1e-06 + squared)
    clipped = combined * (math.sqrt(2 * RANK * D) / grad_norm)
    first = 0.9 * m1_ref[...] + 0.1 * clipped
    second = 0.95 * m2_ref[...] + 0.05 * clipped * clipped
    first_ref[...] = first
    second_ref[...] = second
    step_ref[...] = first / (1.0 - 0.9**20) / (jnp.sqrt(second / (1.0 - 0.95**20)) + 1e-08)


def tail(gram, pieces, moment_one, moment_two):
    tasks = gram.shape[0]
    padded = jnp.zeros((8, 128), jnp.float32).at[:tasks, :tasks].set(gram)
    padded_t = jnp.zeros((8, 128), jnp.float32).at[:tasks, :tasks].set(gram.T)
    out = jax.ShapeDtypeStruct(moment_one.shape, jnp.float32)
    return pl.pallas_call(tail_kernel, out_shape=(out, out, out))(
        padded, padded_t, pieces, moment_one, moment_two
    )


def halve(value, axis, bit):
    me = (lax.axis_index(axis) >> bit) & 1
    size = lax.axis_size(axis)
    halves = value.reshape((2, value.shape[0] // 2) + value.shape[1:])
    mine = lax.dynamic_index_in_dim(halves, me, 0, keepdims=False)
    other = lax.dynamic_index_in_dim(halves, 1 - me, 0, keepdims=False)
    pairs = [(i, i ^ (1 << bit)) for i in range(size)]
    return mine + lax.ppermute(other, axis, pairs)


def butterfly_sum(value, axis):
    size = lax.axis_size(axis)
    step = 1
    while step < size:
        pairs = [(i, i ^ step) for i in range(size)]
        value = value + lax.ppermute(value, axis, pairs)
        step *= 2
    return value


def body(contexts, cotangents, adapter, moment_one, moment_two):
    own_context = contexts[0]
    own_cotangent = cotangents[0]
    rank_width = adapter.shape[1] // 2
    piece = adapter
    for axis in ("z", "x", "core"):
        piece = lax.all_gather(piece, axis, axis=0, tiled=True)
    zs, xs, cs = (lax.axis_size(a) for a in FSDP)
    blocks_in = piece.reshape(cs, xs, zs, -1, piece.shape[1])
    piece = blocks_in.transpose(2, 1, 0, 3, 4).reshape(piece.shape)
    low = jnp.dot(own_context, piece[:, :rank_width], preferred_element_type=jnp.float32).astype(jnp.bfloat16)
    back = jnp.dot(own_cotangent, piece[:, rank_width:], preferred_element_type=jnp.float32).astype(jnp.bfloat16)
    down_part = lax.dot_general(
        own_context, back, (((0,), (0,)), ((), ())), preferred_element_type=jnp.float32
    )
    up_part = lax.dot_general(
        own_cotangent, low, (((0,), (0,)), ((), ())), preferred_element_type=jnp.float32
    )
    grad_rows = jnp.concatenate([down_part, up_part], axis=1)
    full = grad_rows.shape
    grad_rows = grad_rows.reshape(zs, xs, cs, -1, full[1]).transpose(2, 0, 1, 3, 4).reshape(full)
    grad_rows = halve(grad_rows, "core", 0)
    grad_rows = lax.psum_scatter(grad_rows, "z", scatter_dimension=0, tiled=True)
    grad_rows = halve(grad_rows, "x", 1)
    grad_rows = halve(grad_rows, "x", 0)
    tasks = lax.axis_size("task")
    rows, width = grad_rows.shape
    blocks = grad_rows.reshape(rows, tasks, width // tasks).transpose(1, 0, 2)
    pieces = lax.all_to_all(blocks, "task", 0, 0, tiled=True)
    partial_gram = jnp.einsum("sij,tij->st", pieces, pieces, precision=lax.Precision.HIGHEST)
    gram_matrix = partial_gram
    for axis in ALL_AXES:
        gram_matrix = butterfly_sum(gram_matrix, axis)
    return tail(gram_matrix, pieces, moment_one, moment_two)


def solution(mesh):
    tasks, fsdp = mesh.devices.shape
    split = Mesh(mesh.devices.reshape(tasks, fsdp // 8, 4, 2), ("task",) + FSDP)
    in_specs = (
        P("task", FSDP, None),
        P("task", FSDP, None),
        P(FSDP, None),
        P(FSDP, "task"),
        P(FSDP, "task"),
    )
    out_specs = (P(FSDP, "task"), P(FSDP, "task"), P(FSDP, "task"))
    return jax.shard_map(body, mesh=split, in_specs=in_specs, out_specs=out_specs, check_vma=False)
```

```python
import math

import jax
import jax.numpy as jnp
from jax import lax
from jax.experimental import pallas as pl
from jax.sharding import Mesh
from jax.sharding import PartitionSpec as P

D = 4096
RANK = 128
FSDP = ("z", "x", "core")
ALL_AXES = ("core", "x", "z", "task")


def tail_kernel(gram_ref, gramt_ref, pieces_ref, m1_ref, m2_ref, first_ref, second_ref, step_ref):
    gram = gram_ref[...]
    kt = gramt_ref[...]
    shape = gram.shape
    row = lax.broadcasted_iota(jnp.int32, shape, 0)
    lane = lax.broadcasted_iota(jnp.int32, shape, 1)

    def lanes(x):
        return jnp.sum(x, axis=1, keepdims=True)

    def sublanes(x):
        return jnp.sum(x, axis=0, keepdims=True)

    def pick(x, r, l):
        return lanes(sublanes(jnp.where((row == r) & (lane == l), x, 0.0)))

    norm_col = jnp.sqrt(lanes(jnp.where(row == lane, gram, 0.0)))
    k00 = pick(gram, 0, 0)
    n0 = jnp.sqrt(k00)
    k_i0 = sublanes(jnp.where(row == 0, kt, 0.0))
    k_0j = lanes(jnp.where(lane == 0, kt, 0.0))
    system = (k00 - k_i0) / n0 - (k_0j - kt) / norm_col
    right = k00 / n0 - k_0j / norm_col
    aug = jnp.where(lane == 0, right, system)
    tasks = pieces_ref.shape[0]
    for column in range(1, tasks):
        pivot_row = sublanes(jnp.where(row == column, aug, 0.0))
        column_vals = lanes(jnp.where(lane == column, aug, 0.0))
        pivot = lanes(jnp.where(lane[:1] == column, pivot_row, 0.0))
        factor = column_vals / pivot
        aug = jnp.where(row > column, aug - factor * pivot_row, aug)
    answer = [None] * tasks
    lane_row = lax.broadcasted_iota(jnp.int32, (1, shape[1]), 1)
    row_col = lax.broadcasted_iota(jnp.int32, (shape[0], 1), 0)
    for column in reversed(range(1, tasks)):
        pivot_row = sublanes(jnp.where(row == column, aug, 0.0))
        running = lanes(jnp.where(lane_row == 0, pivot_row, 0.0))
        for follow in range(column + 1, tasks):
            running = running - lanes(jnp.where(lane_row == follow, pivot_row, 0.0)) * answer[follow]
        answer[column] = running / lanes(jnp.where(lane_row == column, pivot_row, 0.0))
    total = answer[1]
    for column in range(2, tasks):
        total = total + answer[column]
    answer[0] = 1.0 - total
    alpha_row = jnp.zeros((1, shape[1]), jnp.float32)
    alpha_col = jnp.zeros((shape[0], 1), jnp.float32)
    for t in range(tasks):
        alpha_row = jnp.where(lane_row == t, answer[t], alpha_row)
        alpha_col = jnp.where(row_col == t, answer[t], alpha_col)
    combined = answer[0] * pieces_ref[0]
    for t in range(1, tasks):
        combined = combined + answer[t] * pieces_ref[t]
    squared = sublanes(alpha_col * lanes(gram * alpha_row))
    grad_norm = jnp.sqrt(1e-06 + squared)
    clipped = combined * (math.sqrt(2 * RANK * D) / grad_norm)
    first = 0.9 * m1_ref[...] + 0.1 * clipped
    second = 0.95 * m2_ref[...] + 0.05 * clipped * clipped
    first_ref[...] = first
    second_ref[...] = second
    step_ref[...] = first / (1.0 - 0.9**20) / (jnp.sqrt(second / (1.0 - 0.95**20)) + 1e-08)


def tail(gram, pieces, moment_one, moment_two):
    tasks = gram.shape[0]
    padded = jnp.zeros((8, 128), jnp.float32).at[:tasks, :tasks].set(gram)
    padded_t = jnp.zeros((8, 128), jnp.float32).at[:tasks, :tasks].set(gram.T)
    out = jax.ShapeDtypeStruct(moment_one.shape, jnp.float32)
    return pl.pallas_call(tail_kernel, out_shape=(out, out, out))(
        padded, padded_t, pieces, moment_one, moment_two
    )


def halve(value, axis, bit):
    me = (lax.axis_index(axis) >> bit) & 1
    size = lax.axis_size(axis)
    halves = value.reshape((2, value.shape[0] // 2) + value.shape[1:])
    mine = lax.dynamic_index_in_dim(halves, me, 0, keepdims=False)
    other = lax.dynamic_index_in_dim(halves, 1 - me, 0, keepdims=False)
    pairs = [(i, i ^ (1 << bit)) for i in range(size)]
    return mine + lax.ppermute(other, axis, pairs)


def double(value, axis, bit):
    me = (lax.axis_index(axis) >> bit) & 1
    size = lax.axis_size(axis)
    pairs = [(i, i ^ (1 << bit)) for i in range(size)]
    other = lax.ppermute(value, axis, pairs)
    first = jnp.where(me == 0, value, other)
    second = jnp.where(me == 0, other, value)
    return jnp.concatenate([first, second], axis=0)


def butterfly_sum(value, axis):
    size = lax.axis_size(axis)
    step = 1
    while step < size:
        pairs = [(i, i ^ step) for i in range(size)]
        value = value + lax.ppermute(value, axis, pairs)
        step *= 2
    return value


def body(contexts, cotangents, adapter, moment_one, moment_two):
    own_context = contexts[0]
    own_cotangent = cotangents[0]
    rank_width = adapter.shape[1] // 2
    piece = lax.all_gather(adapter, "z", axis=0, tiled=True)
    piece = double(piece, "x", 0)
    piece = double(piece, "x", 1)
    piece = double(piece, "core", 0)
    zs, xs, cs = (lax.axis_size(a) for a in FSDP)
    blocks_in = piece.reshape(cs, xs, zs, -1, piece.shape[1])
    piece = blocks_in.transpose(2, 1, 0, 3, 4).reshape(piece.shape)
    low = jnp.dot(own_context, piece[:, :rank_width], preferred_element_type=jnp.float32).astype(jnp.bfloat16)
    back = jnp.dot(own_cotangent, piece[:, rank_width:], preferred_element_type=jnp.float32).astype(jnp.bfloat16)
    down_part = lax.dot_general(
        own_context, back, (((0,), (0,)), ((), ())), preferred_element_type=jnp.float32
    )
    up_part = lax.dot_general(
        own_cotangent, low, (((0,), (0,)), ((), ())), preferred_element_type=jnp.float32
    )
    grad_rows = jnp.concatenate([down_part, up_part], axis=1)
    full = grad_rows.shape
    by_core = grad_rows.reshape(zs * xs, cs, -1, full[1])
    me = lax.axis_index("core")
    mine = lax.dynamic_index_in_dim(by_core, me, 1, keepdims=False).reshape(-1, full[1])
    other = lax.dynamic_index_in_dim(by_core, 1 - me, 1, keepdims=False).reshape(-1, full[1])
    grad_rows = mine + lax.ppermute(other, "core", [(0, 1), (1, 0)])
    grad_rows = lax.psum_scatter(grad_rows, "z", scatter_dimension=0, tiled=True)
    grad_rows = halve(grad_rows, "x", 1)
    grad_rows = halve(grad_rows, "x", 0)
    tasks = lax.axis_size("task")
    rows, width = grad_rows.shape
    blocks = grad_rows.reshape(rows, tasks, width // tasks).transpose(1, 0, 2)
    pieces = lax.all_to_all(blocks, "task", 0, 0, tiled=True)
    partial_gram = jnp.einsum("sij,tij->st", pieces, pieces, precision=lax.Precision.HIGHEST)
    gram_matrix = partial_gram
    for axis in ALL_AXES:
        gram_matrix = butterfly_sum(gram_matrix, axis)
    return tail(gram_matrix, pieces, moment_one, moment_two)


def solution(mesh):
    tasks, fsdp = mesh.devices.shape
    split = Mesh(mesh.devices.reshape(tasks, fsdp // 8, 4, 2), ("task",) + FSDP)
    in_specs = (
        P("task", FSDP, None),
        P("task", FSDP, None),
        P(FSDP, None),
        P(FSDP, "task"),
        P(FSDP, "task"),
    )
    out_specs = (P(FSDP, "task"), P(FSDP, "task"), P(FSDP, "task"))
    return jax.shard_map(body, mesh=split, in_specs=in_specs, out_specs=out_specs, check_vma=False)
```

```python
import math

import jax
import jax.numpy as jnp
from jax import lax
from jax.experimental import pallas as pl
from jax.sharding import Mesh
from jax.sharding import PartitionSpec as P

D = 4096
RANK = 128
FSDP = ("z", "x", "core")
ALL_AXES = ("core", "x", "z", "task")


def tail_kernel(gram_ref, gramt_ref, pieces_ref, m1_ref, m2_ref, first_ref, second_ref, step_ref):
    gram = gram_ref[...]
    kt = gramt_ref[...]
    shape = gram.shape
    row = lax.broadcasted_iota(jnp.int32, shape, 0)
    lane = lax.broadcasted_iota(jnp.int32, shape, 1)

    def lanes(x):
        return jnp.sum(x, axis=1, keepdims=True)

    def sublanes(x):
        return jnp.sum(x, axis=0, keepdims=True)

    def pick(x, r, l):
        return lanes(sublanes(jnp.where((row == r) & (lane == l), x, 0.0)))

    norm_col = jnp.sqrt(lanes(jnp.where(row == lane, gram, 0.0)))
    k00 = pick(gram, 0, 0)
    n0 = jnp.sqrt(k00)
    k_i0 = sublanes(jnp.where(row == 0, kt, 0.0))
    k_0j = lanes(jnp.where(lane == 0, kt, 0.0))
    system = (k00 - k_i0) / n0 - (k_0j - kt) / norm_col
    right = k00 / n0 - k_0j / norm_col
    aug = jnp.where(lane == 0, right, system)
    tasks = pieces_ref.shape[0]
    for column in range(1, tasks):
        pivot_row = sublanes(jnp.where(row == column, aug, 0.0))
        column_vals = lanes(jnp.where(lane == column, aug, 0.0))
        pivot = lanes(jnp.where(lane[:1] == column, pivot_row, 0.0))
        factor = column_vals / pivot
        aug = jnp.where(row > column, aug - factor * pivot_row, aug)
    answer = [None] * tasks
    lane_row = lax.broadcasted_iota(jnp.int32, (1, shape[1]), 1)
    row_col = lax.broadcasted_iota(jnp.int32, (shape[0], 1), 0)
    for column in reversed(range(1, tasks)):
        pivot_row = sublanes(jnp.where(row == column, aug, 0.0))
        running = lanes(jnp.where(lane_row == 0, pivot_row, 0.0))
        for follow in range(column + 1, tasks):
            running = running - lanes(jnp.where(lane_row == follow, pivot_row, 0.0)) * answer[follow]
        answer[column] = running / lanes(jnp.where(lane_row == column, pivot_row, 0.0))
    total = answer[1]
    for column in range(2, tasks):
        total = total + answer[column]
    answer[0] = 1.0 - total
    alpha_row = jnp.zeros((1, shape[1]), jnp.float32)
    alpha_col = jnp.zeros((shape[0], 1), jnp.float32)
    for t in range(tasks):
        alpha_row = jnp.where(lane_row == t, answer[t], alpha_row)
        alpha_col = jnp.where(row_col == t, answer[t], alpha_col)
    combined = answer[0] * pieces_ref[0]
    for t in range(1, tasks):
        combined = combined + answer[t] * pieces_ref[t]
    squared = sublanes(alpha_col * lanes(gram * alpha_row))
    grad_norm = jnp.sqrt(1e-06 + squared)
    clipped = combined * (math.sqrt(2 * RANK * D) / grad_norm)
    first = 0.9 * m1_ref[...] + 0.1 * clipped
    second = 0.95 * m2_ref[...] + 0.05 * clipped * clipped
    first_ref[...] = first
    second_ref[...] = second
    step_ref[...] = first / (1.0 - 0.9**20) / (jnp.sqrt(second / (1.0 - 0.95**20)) + 1e-08)


def tail(gram, pieces, moment_one, moment_two):
    tasks = gram.shape[0]
    padded = jnp.zeros((8, 128), jnp.float32).at[:tasks, :tasks].set(gram)
    padded_t = jnp.zeros((8, 128), jnp.float32).at[:tasks, :tasks].set(gram.T)
    out = jax.ShapeDtypeStruct(moment_one.shape, jnp.float32)
    return pl.pallas_call(tail_kernel, out_shape=(out, out, out))(
        padded, padded_t, pieces, moment_one, moment_two
    )


def halve(value, axis, bit):
    me = (lax.axis_index(axis) >> bit) & 1
    size = lax.axis_size(axis)
    halves = value.reshape((2, value.shape[0] // 2) + value.shape[1:])
    mine = lax.dynamic_index_in_dim(halves, me, 0, keepdims=False)
    other = lax.dynamic_index_in_dim(halves, 1 - me, 0, keepdims=False)
    pairs = [(i, i ^ (1 << bit)) for i in range(size)]
    return mine + lax.ppermute(other, axis, pairs)


def double(value, axis, bit):
    me = (lax.axis_index(axis) >> bit) & 1
    size = lax.axis_size(axis)
    pairs = [(i, i ^ (1 << bit)) for i in range(size)]
    other = lax.ppermute(value, axis, pairs)
    first = jnp.where(me == 0, value, other)
    second = jnp.where(me == 0, other, value)
    return jnp.concatenate([first, second], axis=0)


def butterfly_sum(value, axis):
    size = lax.axis_size(axis)
    step = 1
    while step < size:
        pairs = [(i, i ^ step) for i in range(size)]
        value = value + lax.ppermute(value, axis, pairs)
        step *= 2
    return value


def body(contexts, cotangents, adapter, moment_one, moment_two):
    own_context = contexts[0]
    own_cotangent = cotangents[0]
    rank_width = adapter.shape[1] // 2
    piece = lax.all_gather(adapter, "z", axis=0, tiled=True)
    piece = double(piece, "x", 0)
    piece = double(piece, "x", 1)
    piece = double(piece, "core", 0)
    zs, xs, cs = (lax.axis_size(a) for a in FSDP)
    blocks_in = piece.reshape(cs, xs, zs, -1, piece.shape[1])
    piece = blocks_in.transpose(2, 1, 0, 3, 4).reshape(piece.shape)
    low = jnp.dot(own_context, piece[:, :rank_width], preferred_element_type=jnp.float32).astype(jnp.bfloat16)
    back = jnp.dot(own_cotangent, piece[:, rank_width:], preferred_element_type=jnp.float32).astype(jnp.bfloat16)
    down_part = lax.dot_general(
        own_context, back, (((0,), (0,)), ((), ())), preferred_element_type=jnp.float32
    )
    up_part = lax.dot_general(
        own_cotangent, low, (((0,), (0,)), ((), ())), preferred_element_type=jnp.float32
    )
    grad_rows = jnp.concatenate([down_part, up_part], axis=1)
    full = grad_rows.shape
    by_core = grad_rows.reshape(zs * xs, cs, -1, full[1])
    me = lax.axis_index("core")
    mine = lax.dynamic_index_in_dim(by_core, me, 1, keepdims=False).reshape(-1, full[1])
    other = lax.dynamic_index_in_dim(by_core, 1 - me, 1, keepdims=False).reshape(-1, full[1])
    grad_rows = mine + lax.ppermute(other, "core", [(0, 1), (1, 0)])
    grad_rows = lax.psum_scatter(grad_rows, "z", scatter_dimension=0, tiled=True)
    grad_rows = halve(grad_rows, "x", 1)
    grad_rows = halve(grad_rows, "x", 0)
    tasks = lax.axis_size("task")
    rows, width = grad_rows.shape
    blocks = grad_rows.reshape(rows, tasks, width // tasks).transpose(1, 0, 2)
    pieces = lax.all_to_all(blocks, "task", 0, 0, tiled=True)
    partial_gram = jnp.einsum("sij,tij->st", pieces, pieces, precision=lax.Precision.HIGHEST)
    gram_matrix = butterfly_sum(partial_gram, "core")
    for axis in ("x", "z", "task"):
        gathered = lax.all_gather(gram_matrix, axis, axis=0, tiled=False)
        gram_matrix = gathered[0]
        for position in range(1, gathered.shape[0]):
            gram_matrix = gram_matrix + gathered[position]
    return tail(gram_matrix, pieces, moment_one, moment_two)


def solution(mesh):
    tasks, fsdp = mesh.devices.shape
    split = Mesh(mesh.devices.reshape(tasks, fsdp // 8, 4, 2), ("task",) + FSDP)
    in_specs = (
        P("task", FSDP, None),
        P("task", FSDP, None),
        P(FSDP, None),
        P(FSDP, "task"),
        P(FSDP, "task"),
    )
    out_specs = (P(FSDP, "task"), P(FSDP, "task"), P(FSDP, "task"))
    return jax.shard_map(body, mesh=split, in_specs=in_specs, out_specs=out_specs, check_vma=False)
```

```python
import math

import jax
import jax.numpy as jnp
from jax import lax
from jax.experimental import pallas as pl
from jax.sharding import Mesh
from jax.sharding import PartitionSpec as P

D = 4096
RANK = 128
FSDP = ("z", "x", "core")
ALL_AXES = ("core", "x", "z", "task")


def tail_kernel(gram_ref, gramt_ref, pieces_ref, m1_ref, m2_ref, first_ref, second_ref, step_ref):
    gram = gram_ref[...]
    kt = gramt_ref[...]
    shape = gram.shape
    row = lax.broadcasted_iota(jnp.int32, shape, 0)
    lane = lax.broadcasted_iota(jnp.int32, shape, 1)

    def lanes(x):
        return jnp.sum(x, axis=1, keepdims=True)

    def sublanes(x):
        return jnp.sum(x, axis=0, keepdims=True)

    def pick(x, r, l):
        return lanes(sublanes(jnp.where((row == r) & (lane == l), x, 0.0)))

    norm_col = jnp.sqrt(lanes(jnp.where(row == lane, gram, 0.0)))
    k00 = pick(gram, 0, 0)
    n0 = jnp.sqrt(k00)
    k_i0 = sublanes(jnp.where(row == 0, kt, 0.0))
    k_0j = lanes(jnp.where(lane == 0, kt, 0.0))
    system = (k00 - k_i0) / n0 - (k_0j - kt) / norm_col
    right = k00 / n0 - k_0j / norm_col
    aug = jnp.where(lane == 0, right, system)
    tasks = pieces_ref.shape[0]
    for column in range(1, tasks):
        pivot_row = sublanes(jnp.where(row == column, aug, 0.0))
        column_vals = lanes(jnp.where(lane == column, aug, 0.0))
        pivot = lanes(jnp.where(lane[:1] == column, pivot_row, 0.0))
        factor = column_vals / pivot
        aug = jnp.where(row > column, aug - factor * pivot_row, aug)
    answer = [None] * tasks
    lane_row = lax.broadcasted_iota(jnp.int32, (1, shape[1]), 1)
    row_col = lax.broadcasted_iota(jnp.int32, (shape[0], 1), 0)
    for column in reversed(range(1, tasks)):
        pivot_row = sublanes(jnp.where(row == column, aug, 0.0))
        running = lanes(jnp.where(lane_row == 0, pivot_row, 0.0))
        for follow in range(column + 1, tasks):
            running = running - lanes(jnp.where(lane_row == follow, pivot_row, 0.0)) * answer[follow]
        answer[column] = running / lanes(jnp.where(lane_row == column, pivot_row, 0.0))
    total = answer[1]
    for column in range(2, tasks):
        total = total + answer[column]
    answer[0] = 1.0 - total
    alpha_row = jnp.zeros((1, shape[1]), jnp.float32)
    alpha_col = jnp.zeros((shape[0], 1), jnp.float32)
    for t in range(tasks):
        alpha_row = jnp.where(lane_row == t, answer[t], alpha_row)
        alpha_col = jnp.where(row_col == t, answer[t], alpha_col)
    combined = answer[0] * pieces_ref[0]
    for t in range(1, tasks):
        combined = combined + answer[t] * pieces_ref[t]
    squared = sublanes(alpha_col * lanes(gram * alpha_row))
    grad_norm = jnp.sqrt(1e-06 + squared)
    clipped = combined * (math.sqrt(2 * RANK * D) / grad_norm)
    first = 0.9 * m1_ref[...] + 0.1 * clipped
    second = 0.95 * m2_ref[...] + 0.05 * clipped * clipped
    first_ref[...] = first
    second_ref[...] = second
    step_ref[...] = first / (1.0 - 0.9**20) / (jnp.sqrt(second / (1.0 - 0.95**20)) + 1e-08)


def tail(gram, pieces, moment_one, moment_two):
    tasks = gram.shape[0]
    padded = jnp.zeros((8, 128), jnp.float32).at[:tasks, :tasks].set(gram)
    padded_t = jnp.zeros((8, 128), jnp.float32).at[:tasks, :tasks].set(gram.T)
    out = jax.ShapeDtypeStruct(moment_one.shape, jnp.float32)
    return pl.pallas_call(tail_kernel, out_shape=(out, out, out))(
        padded, padded_t, pieces, moment_one, moment_two
    )


def halve(value, axis, bit):
    me = (lax.axis_index(axis) >> bit) & 1
    size = lax.axis_size(axis)
    halves = value.reshape((2, value.shape[0] // 2) + value.shape[1:])
    mine = lax.dynamic_index_in_dim(halves, me, 0, keepdims=False)
    other = lax.dynamic_index_in_dim(halves, 1 - me, 0, keepdims=False)
    pairs = [(i, i ^ (1 << bit)) for i in range(size)]
    return mine + lax.ppermute(other, axis, pairs)


def double(value, axis, bit):
    me = (lax.axis_index(axis) >> bit) & 1
    size = lax.axis_size(axis)
    pairs = [(i, i ^ (1 << bit)) for i in range(size)]
    other = lax.ppermute(value, axis, pairs)
    first = jnp.where(me == 0, value, other)
    second = jnp.where(me == 0, other, value)
    return jnp.concatenate([first, second], axis=0)


def butterfly_sum(value, axis):
    size = lax.axis_size(axis)
    step = 1
    while step < size:
        pairs = [(i, i ^ step) for i in range(size)]
        value = value + lax.ppermute(value, axis, pairs)
        step *= 2
    return value


def body(contexts, cotangents, adapter, moment_one, moment_two):
    own_context = contexts[0]
    own_cotangent = cotangents[0]
    rank_width = adapter.shape[1] // 2
    piece = lax.all_gather(adapter, "z", axis=0, tiled=True)
    piece = double(piece, "x", 0)
    piece = double(piece, "x", 1)
    piece = double(piece, "core", 0)
    zs, xs, cs = (lax.axis_size(a) for a in FSDP)
    blocks_in = piece.reshape(cs, xs, zs, -1, piece.shape[1])
    piece = blocks_in.transpose(2, 1, 0, 3, 4).reshape(piece.shape)
    low = jnp.dot(own_context, piece[:, :rank_width], preferred_element_type=jnp.float32).astype(jnp.bfloat16)
    back = jnp.dot(own_cotangent, piece[:, rank_width:], preferred_element_type=jnp.float32).astype(jnp.bfloat16)
    down_part = lax.dot_general(
        own_context, back, (((0,), (0,)), ((), ())), preferred_element_type=jnp.float32
    )
    up_part = lax.dot_general(
        own_cotangent, low, (((0,), (0,)), ((), ())), preferred_element_type=jnp.float32
    )
    grad_rows = jnp.concatenate([down_part, up_part], axis=1)
    full = grad_rows.shape
    by_core = grad_rows.reshape(zs * xs, cs, -1, full[1])
    me = lax.axis_index("core")
    mine = lax.dynamic_index_in_dim(by_core, me, 1, keepdims=False).reshape(-1, full[1])
    other = lax.dynamic_index_in_dim(by_core, 1 - me, 1, keepdims=False).reshape(-1, full[1])
    grad_rows = mine + lax.ppermute(other, "core", [(0, 1), (1, 0)])
    grad_rows = lax.psum_scatter(grad_rows, "z", scatter_dimension=0, tiled=True)
    tasks = lax.axis_size("task")
    rows, width = grad_rows.shape
    tiles = grad_rows.reshape(xs, rows // xs, tasks, width // tasks).transpose(0, 2, 1, 3)
    tiles = tiles.reshape(xs * tasks, rows // xs, width // tasks)
    tiles = lax.all_to_all(tiles, ("x", "task"), 0, 0, tiled=True)
    tiles = tiles.reshape(xs, tasks, rows // xs, width // tasks)
    pieces = tiles[0]
    for position in range(1, xs):
        pieces = pieces + tiles[position]
    partial_gram = jnp.einsum("sij,tij->st", pieces, pieces, precision=lax.Precision.HIGHEST)
    gram_matrix = butterfly_sum(partial_gram, "core")
    for axis in ("x", "z"):
        gathered = lax.all_gather(gram_matrix, axis, axis=0, tiled=False)
        gram_matrix = gathered[0]
        for position in range(1, gathered.shape[0]):
            gram_matrix = gram_matrix + gathered[position]
    gram_matrix = butterfly_sum(gram_matrix, "task")
    return tail(gram_matrix, pieces, moment_one, moment_two)


def solution(mesh):
    tasks, fsdp = mesh.devices.shape
    split = Mesh(mesh.devices.reshape(tasks, fsdp // 8, 4, 2), ("task",) + FSDP)
    in_specs = (
        P("task", FSDP, None),
        P("task", FSDP, None),
        P(FSDP, None),
        P(FSDP, "task"),
        P(FSDP, "task"),
    )
    out_specs = (P(FSDP, "task"), P(FSDP, "task"), P(FSDP, "task"))
    return jax.shard_map(body, mesh=split, in_specs=in_specs, out_specs=out_specs, check_vma=False)
```

```python
import math

import jax
import jax.numpy as jnp
from jax import lax
from jax.experimental import pallas as pl
from jax.sharding import Mesh
from jax.sharding import PartitionSpec as P

D = 4096
RANK = 128
FSDP = ("z", "x", "core")
ALL_AXES = ("core", "x", "z", "task")


def tail_kernel(gram_ref, gramt_ref, pieces_ref, m1_ref, m2_ref, first_ref, second_ref, step_ref):
    gram = gram_ref[...]
    kt = gramt_ref[...]
    shape = gram.shape
    row = lax.broadcasted_iota(jnp.int32, shape, 0)
    lane = lax.broadcasted_iota(jnp.int32, shape, 1)

    def lanes(x):
        return jnp.sum(x, axis=1, keepdims=True)

    def sublanes(x):
        return jnp.sum(x, axis=0, keepdims=True)

    def pick(x, r, l):
        return lanes(sublanes(jnp.where((row == r) & (lane == l), x, 0.0)))

    norm_col = jnp.sqrt(lanes(jnp.where(row == lane, gram, 0.0)))
    k00 = pick(gram, 0, 0)
    n0 = jnp.sqrt(k00)
    k_i0 = sublanes(jnp.where(row == 0, kt, 0.0))
    k_0j = lanes(jnp.where(lane == 0, kt, 0.0))
    system = (k00 - k_i0) / n0 - (k_0j - kt) / norm_col
    right = k00 / n0 - k_0j / norm_col
    aug = jnp.where(lane == 0, right, system)
    tasks = pieces_ref.shape[0]
    for column in range(1, tasks):
        pivot_row = sublanes(jnp.where(row == column, aug, 0.0))
        column_vals = lanes(jnp.where(lane == column, aug, 0.0))
        pivot = lanes(jnp.where(lane[:1] == column, pivot_row, 0.0))
        factor = column_vals / pivot
        aug = jnp.where(row > column, aug - factor * pivot_row, aug)
    answer = [None] * tasks
    lane_row = lax.broadcasted_iota(jnp.int32, (1, shape[1]), 1)
    row_col = lax.broadcasted_iota(jnp.int32, (shape[0], 1), 0)
    for column in reversed(range(1, tasks)):
        pivot_row = sublanes(jnp.where(row == column, aug, 0.0))
        running = lanes(jnp.where(lane_row == 0, pivot_row, 0.0))
        for follow in range(column + 1, tasks):
            running = running - lanes(jnp.where(lane_row == follow, pivot_row, 0.0)) * answer[follow]
        answer[column] = running / lanes(jnp.where(lane_row == column, pivot_row, 0.0))
    total = answer[1]
    for column in range(2, tasks):
        total = total + answer[column]
    answer[0] = 1.0 - total
    alpha_row = jnp.zeros((1, shape[1]), jnp.float32)
    alpha_col = jnp.zeros((shape[0], 1), jnp.float32)
    for t in range(tasks):
        alpha_row = jnp.where(lane_row == t, answer[t], alpha_row)
        alpha_col = jnp.where(row_col == t, answer[t], alpha_col)
    combined = answer[0] * pieces_ref[0]
    for t in range(1, tasks):
        combined = combined + answer[t] * pieces_ref[t]
    squared = sublanes(alpha_col * lanes(gram * alpha_row))
    grad_norm = jnp.sqrt(1e-06 + squared)
    clipped = combined * (math.sqrt(2 * RANK * D) / grad_norm)
    first = 0.9 * m1_ref[...] + 0.1 * clipped
    second = 0.95 * m2_ref[...] + 0.05 * clipped * clipped
    first_ref[...] = first
    second_ref[...] = second
    step_ref[...] = first / (1.0 - 0.9**20) / (jnp.sqrt(second / (1.0 - 0.95**20)) + 1e-08)


def tail(gram, pieces, moment_one, moment_two):
    tasks = gram.shape[0]
    padded = jnp.zeros((8, 128), jnp.float32).at[:tasks, :tasks].set(gram)
    padded_t = jnp.zeros((8, 128), jnp.float32).at[:tasks, :tasks].set(gram.T)
    out = jax.ShapeDtypeStruct(moment_one.shape, jnp.float32)
    return pl.pallas_call(tail_kernel, out_shape=(out, out, out))(
        padded, padded_t, pieces, moment_one, moment_two
    )


def halve(value, axis, bit):
    me = (lax.axis_index(axis) >> bit) & 1
    size = lax.axis_size(axis)
    halves = value.reshape((2, value.shape[0] // 2) + value.shape[1:])
    mine = lax.dynamic_index_in_dim(halves, me, 0, keepdims=False)
    other = lax.dynamic_index_in_dim(halves, 1 - me, 0, keepdims=False)
    pairs = [(i, i ^ (1 << bit)) for i in range(size)]
    return mine + lax.ppermute(other, axis, pairs)


def double(value, axis, bit):
    me = (lax.axis_index(axis) >> bit) & 1
    size = lax.axis_size(axis)
    pairs = [(i, i ^ (1 << bit)) for i in range(size)]
    other = lax.ppermute(value, axis, pairs)
    first = jnp.where(me == 0, value, other)
    second = jnp.where(me == 0, other, value)
    return jnp.concatenate([first, second], axis=0)


def butterfly_sum(value, axis):
    size = lax.axis_size(axis)
    step = 1
    while step < size:
        pairs = [(i, i ^ step) for i in range(size)]
        value = value + lax.ppermute(value, axis, pairs)
        step *= 2
    return value


def body(contexts, cotangents, adapter, moment_one, moment_two):
    own_context = contexts[0]
    own_cotangent = cotangents[0]
    rank_width = adapter.shape[1] // 2
    zs, xs, cs = (lax.axis_size(a) for a in FSDP)
    fsdp = zs * xs * cs
    piece = jnp.broadcast_to(adapter[None], (fsdp,) + adapter.shape)
    piece = lax.all_to_all(piece, FSDP, 0, 0, tiled=True).reshape(-1, adapter.shape[1])
    low = jnp.dot(own_context, piece[:, :rank_width], preferred_element_type=jnp.float32).astype(jnp.bfloat16)
    back = jnp.dot(own_cotangent, piece[:, rank_width:], preferred_element_type=jnp.float32).astype(jnp.bfloat16)
    down_part = lax.dot_general(
        own_context, back, (((0,), (0,)), ((), ())), preferred_element_type=jnp.float32
    )
    up_part = lax.dot_general(
        own_cotangent, low, (((0,), (0,)), ((), ())), preferred_element_type=jnp.float32
    )
    grad_rows = jnp.concatenate([down_part, up_part], axis=1)
    full = grad_rows.shape
    by_core = grad_rows.reshape(zs * xs, cs, -1, full[1])
    me = lax.axis_index("core")
    mine = lax.dynamic_index_in_dim(by_core, me, 1, keepdims=False).reshape(-1, full[1])
    other = lax.dynamic_index_in_dim(by_core, 1 - me, 1, keepdims=False).reshape(-1, full[1])
    grad_rows = mine + lax.ppermute(other, "core", [(0, 1), (1, 0)])
    grad_rows = lax.psum_scatter(grad_rows, "z", scatter_dimension=0, tiled=True)
    tasks = lax.axis_size("task")
    rows, width = grad_rows.shape
    tiles = grad_rows.reshape(xs, rows // xs, tasks, width // tasks).transpose(0, 2, 1, 3)
    tiles = tiles.reshape(xs * tasks, rows // xs, width // tasks)
    tiles = lax.all_to_all(tiles, ("x", "task"), 0, 0, tiled=True)
    tiles = tiles.reshape(xs, tasks, rows // xs, width // tasks)
    pieces = tiles[0]
    for position in range(1, xs):
        pieces = pieces + tiles[position]
    partial_gram = jnp.einsum("sij,tij->st", pieces, pieces, precision=lax.Precision.HIGHEST)
    devices = fsdp * tasks
    gathered = jnp.broadcast_to(partial_gram[None], (devices,) + partial_gram.shape)
    gathered = lax.all_to_all(gathered, ("task",) + FSDP, 0, 0, tiled=True)
    gram_matrix = jnp.sum(gathered, axis=0)
    return tail(gram_matrix, pieces, moment_one, moment_two)


def solution(mesh):
    tasks, fsdp = mesh.devices.shape
    split = Mesh(mesh.devices.reshape(tasks, fsdp // 8, 4, 2), ("task",) + FSDP)
    in_specs = (
        P("task", FSDP, None),
        P("task", FSDP, None),
        P(FSDP, None),
        P(FSDP, "task"),
        P(FSDP, "task"),
    )
    out_specs = (P(FSDP, "task"), P(FSDP, "task"), P(FSDP, "task"))
    return jax.shard_map(body, mesh=split, in_specs=in_specs, out_specs=out_specs, check_vma=False)
```

```python
import math

import jax
import jax.numpy as jnp
from jax import lax
from jax.experimental import pallas as pl
from jax.sharding import Mesh
from jax.sharding import PartitionSpec as P

D = 4096
RANK = 128
FSDP = ("z", "x", "core")
ALL_AXES = ("core", "x", "z", "task")


def tail_kernel(gram_ref, gramt_ref, pieces_ref, m1_ref, m2_ref, first_ref, second_ref, step_ref):
    gram = gram_ref[...]
    kt = gramt_ref[...]
    shape = gram.shape
    row = lax.broadcasted_iota(jnp.int32, shape, 0)
    lane = lax.broadcasted_iota(jnp.int32, shape, 1)

    def lanes(x):
        return jnp.sum(x, axis=1, keepdims=True)

    def sublanes(x):
        return jnp.sum(x, axis=0, keepdims=True)

    def pick(x, r, l):
        return lanes(sublanes(jnp.where((row == r) & (lane == l), x, 0.0)))

    norm_col = jnp.sqrt(lanes(jnp.where(row == lane, gram, 0.0)))
    k00 = pick(gram, 0, 0)
    n0 = jnp.sqrt(k00)
    k_i0 = sublanes(jnp.where(row == 0, kt, 0.0))
    k_0j = lanes(jnp.where(lane == 0, kt, 0.0))
    system = (k00 - k_i0) / n0 - (k_0j - kt) / norm_col
    right = k00 / n0 - k_0j / norm_col
    aug = jnp.where(lane == 0, right, system)
    tasks = pieces_ref.shape[0]
    for column in range(1, tasks):
        pivot_row = sublanes(jnp.where(row == column, aug, 0.0))
        column_vals = lanes(jnp.where(lane == column, aug, 0.0))
        pivot = lanes(jnp.where(lane[:1] == column, pivot_row, 0.0))
        factor = column_vals / pivot
        aug = jnp.where(row > column, aug - factor * pivot_row, aug)
    answer = [None] * tasks
    lane_row = lax.broadcasted_iota(jnp.int32, (1, shape[1]), 1)
    row_col = lax.broadcasted_iota(jnp.int32, (shape[0], 1), 0)
    for column in reversed(range(1, tasks)):
        pivot_row = sublanes(jnp.where(row == column, aug, 0.0))
        running = lanes(jnp.where(lane_row == 0, pivot_row, 0.0))
        for follow in range(column + 1, tasks):
            running = running - lanes(jnp.where(lane_row == follow, pivot_row, 0.0)) * answer[follow]
        answer[column] = running / lanes(jnp.where(lane_row == column, pivot_row, 0.0))
    total = answer[1]
    for column in range(2, tasks):
        total = total + answer[column]
    answer[0] = 1.0 - total
    alpha_row = jnp.zeros((1, shape[1]), jnp.float32)
    alpha_col = jnp.zeros((shape[0], 1), jnp.float32)
    for t in range(tasks):
        alpha_row = jnp.where(lane_row == t, answer[t], alpha_row)
        alpha_col = jnp.where(row_col == t, answer[t], alpha_col)
    combined = answer[0] * pieces_ref[0]
    for t in range(1, tasks):
        combined = combined + answer[t] * pieces_ref[t]
    squared = sublanes(alpha_col * lanes(gram * alpha_row))
    grad_norm = jnp.sqrt(1e-06 + squared)
    clipped = combined * (math.sqrt(2 * RANK * D) / grad_norm)
    first = 0.9 * m1_ref[...] + 0.1 * clipped
    second = 0.95 * m2_ref[...] + 0.05 * clipped * clipped
    first_ref[...] = first
    second_ref[...] = second
    step_ref[...] = first / (1.0 - 0.9**20) / (jnp.sqrt(second / (1.0 - 0.95**20)) + 1e-08)


def tail(gram, pieces, moment_one, moment_two):
    tasks = gram.shape[0]
    padded = jnp.zeros((8, 128), jnp.float32).at[:tasks, :tasks].set(gram)
    padded_t = jnp.zeros((8, 128), jnp.float32).at[:tasks, :tasks].set(gram.T)
    out = jax.ShapeDtypeStruct(moment_one.shape, jnp.float32)
    return pl.pallas_call(tail_kernel, out_shape=(out, out, out))(
        padded, padded_t, pieces, moment_one, moment_two
    )


def halve(value, axis, bit):
    me = (lax.axis_index(axis) >> bit) & 1
    size = lax.axis_size(axis)
    halves = value.reshape((2, value.shape[0] // 2) + value.shape[1:])
    mine = lax.dynamic_index_in_dim(halves, me, 0, keepdims=False)
    other = lax.dynamic_index_in_dim(halves, 1 - me, 0, keepdims=False)
    pairs = [(i, i ^ (1 << bit)) for i in range(size)]
    return mine + lax.ppermute(other, axis, pairs)


def double(value, axis, bit):
    me = (lax.axis_index(axis) >> bit) & 1
    size = lax.axis_size(axis)
    pairs = [(i, i ^ (1 << bit)) for i in range(size)]
    other = lax.ppermute(value, axis, pairs)
    first = jnp.where(me == 0, value, other)
    second = jnp.where(me == 0, other, value)
    return jnp.concatenate([first, second], axis=0)


def gather_rows(value, axis):
    size = lax.axis_size(axis)
    copies = jnp.broadcast_to(value[None], (size,) + value.shape)
    return lax.all_to_all(copies, axis, 0, 0, tiled=True)


def butterfly_sum(value, axis):
    size = lax.axis_size(axis)
    step = 1
    while step < size:
        pairs = [(i, i ^ step) for i in range(size)]
        value = value + lax.ppermute(value, axis, pairs)
        step *= 2
    return value


def body(contexts, cotangents, adapter, moment_one, moment_two):
    own_context = contexts[0]
    own_cotangent = cotangents[0]
    rank_width = adapter.shape[1] // 2
    piece = gather_rows(adapter, "z")
    piece = gather_rows(piece, "x").reshape(-1, adapter.shape[1])
    piece = double(piece, "core", 0)
    zs, xs, cs = (lax.axis_size(a) for a in FSDP)
    blocks_in = piece.reshape(cs, xs, zs, -1, piece.shape[1])
    piece = blocks_in.transpose(2, 1, 0, 3, 4).reshape(piece.shape)
    low = jnp.dot(own_context, piece[:, :rank_width], preferred_element_type=jnp.float32).astype(jnp.bfloat16)
    back = jnp.dot(own_cotangent, piece[:, rank_width:], preferred_element_type=jnp.float32).astype(jnp.bfloat16)
    down_part = lax.dot_general(
        own_context, back, (((0,), (0,)), ((), ())), preferred_element_type=jnp.float32
    )
    up_part = lax.dot_general(
        own_cotangent, low, (((0,), (0,)), ((), ())), preferred_element_type=jnp.float32
    )
    grad_rows = jnp.concatenate([down_part, up_part], axis=1)
    full = grad_rows.shape
    by_core = grad_rows.reshape(zs * xs, cs, -1, full[1])
    me = lax.axis_index("core")
    mine = lax.dynamic_index_in_dim(by_core, me, 1, keepdims=False).reshape(-1, full[1])
    other = lax.dynamic_index_in_dim(by_core, 1 - me, 1, keepdims=False).reshape(-1, full[1])
    grad_rows = mine + lax.ppermute(other, "core", [(0, 1), (1, 0)])
    grad_rows = lax.psum_scatter(grad_rows, "z", scatter_dimension=0, tiled=True)
    tasks = lax.axis_size("task")
    rows, width = grad_rows.shape
    tiles = grad_rows.reshape(xs, rows // xs, tasks, width // tasks).transpose(0, 2, 1, 3)
    tiles = tiles.reshape(xs * tasks, rows // xs, width // tasks)
    tiles = lax.all_to_all(tiles, ("x", "task"), 0, 0, tiled=True)
    tiles = tiles.reshape(xs, tasks, rows // xs, width // tasks)
    pieces = tiles[0]
    for position in range(1, xs):
        pieces = pieces + tiles[position]
    partial_gram = jnp.einsum("sij,tij->st", pieces, pieces, precision=lax.Precision.HIGHEST)
    gram_matrix = butterfly_sum(partial_gram, "core")
    for axis in ("x", "z"):
        gathered = gather_rows(gram_matrix, axis)
        gram_matrix = gathered[0]
        for position in range(1, gathered.shape[0]):
            gram_matrix = gram_matrix + gathered[position]
    gram_matrix = butterfly_sum(gram_matrix, "task")
    return tail(gram_matrix, pieces, moment_one, moment_two)


def solution(mesh):
    tasks, fsdp = mesh.devices.shape
    split = Mesh(mesh.devices.reshape(tasks, fsdp // 8, 4, 2), ("task",) + FSDP)
    in_specs = (
        P("task", FSDP, None),
        P("task", FSDP, None),
        P(FSDP, None),
        P(FSDP, "task"),
        P(FSDP, "task"),
    )
    out_specs = (P(FSDP, "task"), P(FSDP, "task"), P(FSDP, "task"))
    return jax.shard_map(body, mesh=split, in_specs=in_specs, out_specs=out_specs, check_vma=False)
```

```python
import math

import jax
import jax.numpy as jnp
from jax import lax
from jax.experimental import pallas as pl
from jax.sharding import Mesh
from jax.sharding import PartitionSpec as P

D = 4096
RANK = 128
FSDP = ("z", "x", "core")
ALL_AXES = ("core", "x", "z", "task")


def tail_kernel(gram_ref, gramt_ref, pieces_ref, m1_ref, m2_ref, first_ref, second_ref, step_ref):
    gram = gram_ref[...]
    kt = gramt_ref[...]
    shape = gram.shape
    row = lax.broadcasted_iota(jnp.int32, shape, 0)
    lane = lax.broadcasted_iota(jnp.int32, shape, 1)

    def lanes(x):
        return jnp.sum(x, axis=1, keepdims=True)

    def sublanes(x):
        return jnp.sum(x, axis=0, keepdims=True)

    def pick(x, r, l):
        return lanes(sublanes(jnp.where((row == r) & (lane == l), x, 0.0)))

    norm_col = jnp.sqrt(lanes(jnp.where(row == lane, gram, 0.0)))
    k00 = pick(gram, 0, 0)
    n0 = jnp.sqrt(k00)
    k_i0 = sublanes(jnp.where(row == 0, kt, 0.0))
    k_0j = lanes(jnp.where(lane == 0, kt, 0.0))
    system = (k00 - k_i0) / n0 - (k_0j - kt) / norm_col
    right = k00 / n0 - k_0j / norm_col
    aug = jnp.where(lane == 0, right, system)
    tasks = pieces_ref.shape[0]
    for column in range(1, tasks):
        pivot_row = sublanes(jnp.where(row == column, aug, 0.0))
        column_vals = lanes(jnp.where(lane == column, aug, 0.0))
        pivot = lanes(jnp.where(lane[:1] == column, pivot_row, 0.0))
        factor = column_vals / pivot
        aug = jnp.where(row > column, aug - factor * pivot_row, aug)
    answer = [None] * tasks
    lane_row = lax.broadcasted_iota(jnp.int32, (1, shape[1]), 1)
    row_col = lax.broadcasted_iota(jnp.int32, (shape[0], 1), 0)
    for column in reversed(range(1, tasks)):
        pivot_row = sublanes(jnp.where(row == column, aug, 0.0))
        running = lanes(jnp.where(lane_row == 0, pivot_row, 0.0))
        for follow in range(column + 1, tasks):
            running = running - lanes(jnp.where(lane_row == follow, pivot_row, 0.0)) * answer[follow]
        answer[column] = running / lanes(jnp.where(lane_row == column, pivot_row, 0.0))
    total = answer[1]
    for column in range(2, tasks):
        total = total + answer[column]
    answer[0] = 1.0 - total
    alpha_row = jnp.zeros((1, shape[1]), jnp.float32)
    alpha_col = jnp.zeros((shape[0], 1), jnp.float32)
    for t in range(tasks):
        alpha_row = jnp.where(lane_row == t, answer[t], alpha_row)
        alpha_col = jnp.where(row_col == t, answer[t], alpha_col)
    combined = answer[0] * pieces_ref[0]
    for t in range(1, tasks):
        combined = combined + answer[t] * pieces_ref[t]
    squared = sublanes(alpha_col * lanes(gram * alpha_row))
    grad_norm = jnp.sqrt(1e-06 + squared)
    clipped = combined * (math.sqrt(2 * RANK * D) / grad_norm)
    first = 0.9 * m1_ref[...] + 0.1 * clipped
    second = 0.95 * m2_ref[...] + 0.05 * clipped * clipped
    first_ref[...] = first
    second_ref[...] = second
    step_ref[...] = first / (1.0 - 0.9**20) / (jnp.sqrt(second / (1.0 - 0.95**20)) + 1e-08)


def tail(gram, pieces, moment_one, moment_two):
    tasks = gram.shape[0]
    padded = jnp.zeros((8, 128), jnp.float32).at[:tasks, :tasks].set(gram)
    padded_t = jnp.zeros((8, 128), jnp.float32).at[:tasks, :tasks].set(gram.T)
    out = jax.ShapeDtypeStruct(moment_one.shape, jnp.float32)
    return pl.pallas_call(tail_kernel, out_shape=(out, out, out))(
        padded, padded_t, pieces, moment_one, moment_two
    )


def halve(value, axis, bit):
    me = (lax.axis_index(axis) >> bit) & 1
    size = lax.axis_size(axis)
    halves = value.reshape((2, value.shape[0] // 2) + value.shape[1:])
    mine = lax.dynamic_index_in_dim(halves, me, 0, keepdims=False)
    other = lax.dynamic_index_in_dim(halves, 1 - me, 0, keepdims=False)
    pairs = [(i, i ^ (1 << bit)) for i in range(size)]
    return mine + lax.ppermute(other, axis, pairs)


def double(value, axis, bit):
    me = (lax.axis_index(axis) >> bit) & 1
    size = lax.axis_size(axis)
    pairs = [(i, i ^ (1 << bit)) for i in range(size)]
    other = lax.ppermute(value, axis, pairs)
    first = jnp.where(me == 0, value, other)
    second = jnp.where(me == 0, other, value)
    return jnp.concatenate([first, second], axis=0)


def gather_rows(value, axis):
    size = lax.axis_size(axis)
    copies = jnp.broadcast_to(value[None], (size,) + value.shape)
    return lax.all_to_all(copies, axis, 0, 0, tiled=True)


def butterfly_sum(value, axis):
    size = lax.axis_size(axis)
    step = 1
    while step < size:
        pairs = [(i, i ^ step) for i in range(size)]
        value = value + lax.ppermute(value, axis, pairs)
        step *= 2
    return value


def body(contexts, cotangents, adapter, moment_one, moment_two):
    own_context = contexts[0]
    own_cotangent = cotangents[0]
    rank_width = adapter.shape[1] // 2
    piece = gather_rows(adapter, "z")
    piece = gather_rows(piece, "x").reshape(-1, adapter.shape[1])
    piece = double(piece, "core", 0)
    zs, xs, cs = (lax.axis_size(a) for a in FSDP)
    blocks_in = piece.reshape(cs, xs, zs, -1, piece.shape[1])
    piece = blocks_in.transpose(2, 1, 0, 3, 4).reshape(piece.shape)
    low = jnp.dot(own_context, piece[:, :rank_width], preferred_element_type=jnp.float32).astype(jnp.bfloat16)
    back = jnp.dot(own_cotangent, piece[:, rank_width:], preferred_element_type=jnp.float32).astype(jnp.bfloat16)
    down_part = lax.dot_general(
        own_context, back, (((0,), (0,)), ((), ())), preferred_element_type=jnp.float32
    )
    up_part = lax.dot_general(
        own_cotangent, low, (((0,), (0,)), ((), ())), preferred_element_type=jnp.float32
    )
    grad_rows = jnp.concatenate([down_part, up_part], axis=1)
    full = grad_rows.shape
    by_core = grad_rows.reshape(zs * xs, cs, -1, full[1])
    me = lax.axis_index("core")
    mine = lax.dynamic_index_in_dim(by_core, me, 1, keepdims=False).reshape(-1, full[1])
    other = lax.dynamic_index_in_dim(by_core, 1 - me, 1, keepdims=False).reshape(-1, full[1])
    grad_rows = mine + lax.ppermute(other, "core", [(0, 1), (1, 0)])
    chunks = grad_rows.reshape((zs, -1) + grad_rows.shape[1:])
    chunks = lax.all_to_all(chunks, "z", 0, 0, tiled=True)
    grad_rows = chunks[0]
    for position in range(1, zs):
        grad_rows = grad_rows + chunks[position]
    tasks = lax.axis_size("task")
    rows, width = grad_rows.shape
    tiles = grad_rows.reshape(xs, rows // xs, tasks, width // tasks).transpose(0, 2, 1, 3)
    tiles = tiles.reshape(xs * tasks, rows // xs, width // tasks)
    tiles = lax.all_to_all(tiles, ("x", "task"), 0, 0, tiled=True)
    tiles = tiles.reshape(xs, tasks, rows // xs, width // tasks)
    pieces = tiles[0]
    for position in range(1, xs):
        pieces = pieces + tiles[position]
    partial_gram = jnp.einsum("sij,tij->st", pieces, pieces, precision=lax.Precision.HIGHEST)
    gram_matrix = butterfly_sum(partial_gram, "core")
    for axis in ("x", "z"):
        gathered = gather_rows(gram_matrix, axis)
        gram_matrix = gathered[0]
        for position in range(1, gathered.shape[0]):
            gram_matrix = gram_matrix + gathered[position]
    gram_matrix = butterfly_sum(gram_matrix, "task")
    return tail(gram_matrix, pieces, moment_one, moment_two)


def solution(mesh):
    tasks, fsdp = mesh.devices.shape
    split = Mesh(mesh.devices.reshape(tasks, fsdp // 8, 4, 2), ("task",) + FSDP)
    in_specs = (
        P("task", FSDP, None),
        P("task", FSDP, None),
        P(FSDP, None),
        P(FSDP, "task"),
        P(FSDP, "task"),
    )
    out_specs = (P(FSDP, "task"), P(FSDP, "task"), P(FSDP, "task"))
    return jax.shard_map(body, mesh=split, in_specs=in_specs, out_specs=out_specs, check_vma=False)
```

```python
import math

import jax
import jax.numpy as jnp
from jax import lax
from jax.experimental import pallas as pl
from jax.sharding import Mesh
from jax.sharding import PartitionSpec as P

D = 4096
RANK = 128
FSDP = ("z", "x", "core")
ALL_AXES = ("core", "x", "z", "task")


def tail_kernel(gram_ref, gramt_ref, pieces_ref, m1_ref, m2_ref, first_ref, second_ref, step_ref):
    gram = gram_ref[...]
    kt = gramt_ref[...]
    shape = gram.shape
    row = lax.broadcasted_iota(jnp.int32, shape, 0)
    lane = lax.broadcasted_iota(jnp.int32, shape, 1)

    def lanes(x):
        return jnp.sum(x, axis=1, keepdims=True)

    def sublanes(x):
        return jnp.sum(x, axis=0, keepdims=True)

    def pick(x, r, l):
        return lanes(sublanes(jnp.where((row == r) & (lane == l), x, 0.0)))

    norm_col = jnp.sqrt(lanes(jnp.where(row == lane, gram, 0.0)))
    k00 = pick(gram, 0, 0)
    n0 = jnp.sqrt(k00)
    k_i0 = sublanes(jnp.where(row == 0, kt, 0.0))
    k_0j = lanes(jnp.where(lane == 0, kt, 0.0))
    system = (k00 - k_i0) / n0 - (k_0j - kt) / norm_col
    right = k00 / n0 - k_0j / norm_col
    aug = jnp.where(lane == 0, right, system)
    tasks = pieces_ref.shape[0]
    for column in range(1, tasks):
        pivot_row = sublanes(jnp.where(row == column, aug, 0.0))
        column_vals = lanes(jnp.where(lane == column, aug, 0.0))
        pivot = lanes(jnp.where(lane[:1] == column, pivot_row, 0.0))
        factor = column_vals / pivot
        aug = jnp.where(row > column, aug - factor * pivot_row, aug)
    answer = [None] * tasks
    lane_row = lax.broadcasted_iota(jnp.int32, (1, shape[1]), 1)
    row_col = lax.broadcasted_iota(jnp.int32, (shape[0], 1), 0)
    for column in reversed(range(1, tasks)):
        pivot_row = sublanes(jnp.where(row == column, aug, 0.0))
        running = lanes(jnp.where(lane_row == 0, pivot_row, 0.0))
        for follow in range(column + 1, tasks):
            running = running - lanes(jnp.where(lane_row == follow, pivot_row, 0.0)) * answer[follow]
        answer[column] = running / lanes(jnp.where(lane_row == column, pivot_row, 0.0))
    total = answer[1]
    for column in range(2, tasks):
        total = total + answer[column]
    answer[0] = 1.0 - total
    alpha_row = jnp.zeros((1, shape[1]), jnp.float32)
    alpha_col = jnp.zeros((shape[0], 1), jnp.float32)
    for t in range(tasks):
        alpha_row = jnp.where(lane_row == t, answer[t], alpha_row)
        alpha_col = jnp.where(row_col == t, answer[t], alpha_col)
    combined = answer[0] * pieces_ref[0]
    for t in range(1, tasks):
        combined = combined + answer[t] * pieces_ref[t]
    squared = sublanes(alpha_col * lanes(gram * alpha_row))
    grad_norm = jnp.sqrt(1e-06 + squared)
    clipped = combined * (math.sqrt(2 * RANK * D) / grad_norm)
    first = 0.9 * m1_ref[...] + 0.1 * clipped
    second = 0.95 * m2_ref[...] + 0.05 * clipped * clipped
    first_ref[...] = first
    second_ref[...] = second
    step_ref[...] = first / (1.0 - 0.9**20) / (jnp.sqrt(second / (1.0 - 0.95**20)) + 1e-08)


def tail(gram, pieces, moment_one, moment_two):
    tasks = gram.shape[0]
    padded = jnp.zeros((8, 128), jnp.float32).at[:tasks, :tasks].set(gram)
    padded_t = jnp.zeros((8, 128), jnp.float32).at[:tasks, :tasks].set(gram.T)
    out = jax.ShapeDtypeStruct(moment_one.shape, jnp.float32)
    return pl.pallas_call(tail_kernel, out_shape=(out, out, out))(
        padded, padded_t, pieces, moment_one, moment_two
    )


def halve(value, axis, bit):
    me = (lax.axis_index(axis) >> bit) & 1
    size = lax.axis_size(axis)
    halves = value.reshape((2, value.shape[0] // 2) + value.shape[1:])
    mine = lax.dynamic_index_in_dim(halves, me, 0, keepdims=False)
    other = lax.dynamic_index_in_dim(halves, 1 - me, 0, keepdims=False)
    pairs = [(i, i ^ (1 << bit)) for i in range(size)]
    return mine + lax.ppermute(other, axis, pairs)


def double(value, axis, bit):
    me = (lax.axis_index(axis) >> bit) & 1
    size = lax.axis_size(axis)
    pairs = [(i, i ^ (1 << bit)) for i in range(size)]
    other = lax.ppermute(value, axis, pairs)
    first = jnp.where(me == 0, value, other)
    second = jnp.where(me == 0, other, value)
    return jnp.concatenate([first, second], axis=0)


def gather_rows(value, axis):
    size = lax.axis_size(axis)
    copies = jnp.broadcast_to(value[None], (size,) + value.shape)
    return lax.all_to_all(copies, axis, 0, 0, tiled=True)


def butterfly_sum(value, axis):
    size = lax.axis_size(axis)
    step = 1
    while step < size:
        pairs = [(i, i ^ step) for i in range(size)]
        value = value + lax.ppermute(value, axis, pairs)
        step *= 2
    return value


def body(contexts, cotangents, adapter, moment_one, moment_two):
    own_context = contexts[0]
    own_cotangent = cotangents[0]
    rank_width = adapter.shape[1] // 2
    piece = gather_rows(adapter, "z")
    piece = gather_rows(piece, "x").reshape(-1, adapter.shape[1])
    piece = double(piece, "core", 0)
    zs, xs, cs = (lax.axis_size(a) for a in FSDP)
    blocks_in = piece.reshape(cs, xs, zs, -1, piece.shape[1])
    piece = blocks_in.transpose(2, 1, 0, 3, 4).reshape(piece.shape)
    low = jnp.dot(own_context, piece[:, :rank_width], preferred_element_type=jnp.float32).astype(jnp.bfloat16)
    back = jnp.dot(own_cotangent, piece[:, rank_width:], preferred_element_type=jnp.float32).astype(jnp.bfloat16)
    down_part = lax.dot_general(
        own_context, back, (((0,), (0,)), ((), ())), preferred_element_type=jnp.float32
    )
    up_part = lax.dot_general(
        own_cotangent, low, (((0,), (0,)), ((), ())), preferred_element_type=jnp.float32
    )
    grad_rows = jnp.concatenate([down_part, up_part], axis=1)
    full = grad_rows.shape
    by_core = grad_rows.reshape(zs * xs, cs, -1, full[1])
    me = lax.axis_index("core")
    mine = lax.dynamic_index_in_dim(by_core, me, 1, keepdims=False).reshape(-1, full[1])
    other = lax.dynamic_index_in_dim(by_core, 1 - me, 1, keepdims=False).reshape(-1, full[1])
    grad_rows = mine + lax.ppermute(other, "core", [(0, 1), (1, 0)])
    grad_rows = lax.psum_scatter(grad_rows, "z", scatter_dimension=0, tiled=True)
    tasks = lax.axis_size("task")
    rows, width = grad_rows.shape
    tiles = grad_rows.reshape(xs, rows // xs, tasks, width // tasks).transpose(0, 2, 1, 3)
    tiles = tiles.reshape(xs * tasks, rows // xs, width // tasks)
    tiles = lax.all_to_all(tiles, ("x", "task"), 0, 0, tiled=True)
    tiles = tiles.reshape(xs, tasks, rows // xs, width // tasks)
    pieces = tiles[0]
    for position in range(1, xs):
        pieces = pieces + tiles[position]
    partial_gram = jnp.einsum("sij,tij->st", pieces, pieces, precision=lax.Precision.HIGHEST)
    gram_matrix = butterfly_sum(partial_gram, "core")
    for axis in ("x", "z", "task"):
        gathered = gather_rows(gram_matrix, axis)
        gram_matrix = gathered[0]
        for position in range(1, gathered.shape[0]):
            gram_matrix = gram_matrix + gathered[position]
    return tail(gram_matrix, pieces, moment_one, moment_two)


def solution(mesh):
    tasks, fsdp = mesh.devices.shape
    split = Mesh(mesh.devices.reshape(tasks, fsdp // 8, 4, 2), ("task",) + FSDP)
    in_specs = (
        P("task", FSDP, None),
        P("task", FSDP, None),
        P(FSDP, None),
        P(FSDP, "task"),
        P(FSDP, "task"),
    )
    out_specs = (P(FSDP, "task"), P(FSDP, "task"), P(FSDP, "task"))
    return jax.shard_map(body, mesh=split, in_specs=in_specs, out_specs=out_specs, check_vma=False)
```

```python
import math

import jax
import jax.numpy as jnp
from jax import lax
from jax.experimental import pallas as pl
from jax.sharding import Mesh
from jax.sharding import PartitionSpec as P

D = 4096
RANK = 128
FSDP = ("zh", "zl", "x", "core")
Z = ("zh", "zl")


def tail_kernel(gram_ref, gramt_ref, pieces_ref, m1_ref, m2_ref, first_ref, second_ref, step_ref):
    gram = gram_ref[...]
    kt = gramt_ref[...]
    shape = gram.shape
    row = lax.broadcasted_iota(jnp.int32, shape, 0)
    lane = lax.broadcasted_iota(jnp.int32, shape, 1)

    def lanes(x):
        return jnp.sum(x, axis=1, keepdims=True)

    def sublanes(x):
        return jnp.sum(x, axis=0, keepdims=True)

    def pick(x, r, l):
        return lanes(sublanes(jnp.where((row == r) & (lane == l), x, 0.0)))

    norm_col = jnp.sqrt(lanes(jnp.where(row == lane, gram, 0.0)))
    k00 = pick(gram, 0, 0)
    n0 = jnp.sqrt(k00)
    k_i0 = sublanes(jnp.where(row == 0, kt, 0.0))
    k_0j = lanes(jnp.where(lane == 0, kt, 0.0))
    system = (k00 - k_i0) / n0 - (k_0j - kt) / norm_col
    right = k00 / n0 - k_0j / norm_col
    aug = jnp.where(lane == 0, right, system)
    tasks = pieces_ref.shape[0]
    for column in range(1, tasks):
        pivot_row = sublanes(jnp.where(row == column, aug, 0.0))
        column_vals = lanes(jnp.where(lane == column, aug, 0.0))
        pivot = lanes(jnp.where(lane[:1] == column, pivot_row, 0.0))
        factor = column_vals / pivot
        aug = jnp.where(row > column, aug - factor * pivot_row, aug)
    answer = [None] * tasks
    lane_row = lax.broadcasted_iota(jnp.int32, (1, shape[1]), 1)
    row_col = lax.broadcasted_iota(jnp.int32, (shape[0], 1), 0)
    for column in reversed(range(1, tasks)):
        pivot_row = sublanes(jnp.where(row == column, aug, 0.0))
        running = lanes(jnp.where(lane_row == 0, pivot_row, 0.0))
        for follow in range(column + 1, tasks):
            running = running - lanes(jnp.where(lane_row == follow, pivot_row, 0.0)) * answer[follow]
        answer[column] = running / lanes(jnp.where(lane_row == column, pivot_row, 0.0))
    total = answer[1]
    for column in range(2, tasks):
        total = total + answer[column]
    answer[0] = 1.0 - total
    alpha_row = jnp.zeros((1, shape[1]), jnp.float32)
    alpha_col = jnp.zeros((shape[0], 1), jnp.float32)
    for t in range(tasks):
        alpha_row = jnp.where(lane_row == t, answer[t], alpha_row)
        alpha_col = jnp.where(row_col == t, answer[t], alpha_col)
    combined = answer[0] * pieces_ref[0]
    for t in range(1, tasks):
        combined = combined + answer[t] * pieces_ref[t]
    squared = sublanes(alpha_col * lanes(gram * alpha_row))
    grad_norm = jnp.sqrt(1e-06 + squared)
    clipped = combined * (math.sqrt(2 * RANK * D) / grad_norm)
    first = 0.9 * m1_ref[...] + 0.1 * clipped
    second = 0.95 * m2_ref[...] + 0.05 * clipped * clipped
    first_ref[...] = first
    second_ref[...] = second
    step_ref[...] = first / (1.0 - 0.9**20) / (jnp.sqrt(second / (1.0 - 0.95**20)) + 1e-08)


def tail(gram, pieces, moment_one, moment_two):
    tasks = gram.shape[0]
    padded = jnp.zeros((8, 128), jnp.float32).at[:tasks, :tasks].set(gram)
    padded_t = jnp.zeros((8, 128), jnp.float32).at[:tasks, :tasks].set(gram.T)
    out = jax.ShapeDtypeStruct(moment_one.shape, jnp.float32)
    return pl.pallas_call(tail_kernel, out_shape=(out, out, out))(
        padded, padded_t, pieces, moment_one, moment_two
    )


def halve(value, axis, bit):
    me = (lax.axis_index(axis) >> bit) & 1
    size = lax.axis_size(axis)
    halves = value.reshape((2, value.shape[0] // 2) + value.shape[1:])
    mine = lax.dynamic_index_in_dim(halves, me, 0, keepdims=False)
    other = lax.dynamic_index_in_dim(halves, 1 - me, 0, keepdims=False)
    pairs = [(i, i ^ (1 << bit)) for i in range(size)]
    return mine + lax.ppermute(other, axis, pairs)


def double(value, axis, bit):
    me = (lax.axis_index(axis) >> bit) & 1
    size = lax.axis_size(axis)
    pairs = [(i, i ^ (1 << bit)) for i in range(size)]
    other = lax.ppermute(value, axis, pairs)
    first = jnp.where(me == 0, value, other)
    second = jnp.where(me == 0, other, value)
    return jnp.concatenate([first, second], axis=0)


def gather_rows(value, axis):
    size = lax.axis_size(axis)
    copies = jnp.broadcast_to(value[None], (size,) + value.shape)
    return lax.all_to_all(copies, axis, 0, 0, tiled=True)


def butterfly_sum(value, axis):
    size = lax.axis_size(axis)
    step = 1
    while step < size:
        pairs = [(i, i ^ step) for i in range(size)]
        value = value + lax.ppermute(value, axis, pairs)
        step *= 2
    return value


def body(contexts, cotangents, adapter, moment_one, moment_two):
    own_context = contexts[0]
    own_cotangent = cotangents[0]
    rank_width = adapter.shape[1] // 2
    piece = gather_rows(adapter, "zl")
    piece = gather_rows(piece, "zh").reshape((-1,) + adapter.shape)
    piece = gather_rows(piece, "x").reshape(-1, adapter.shape[1])
    piece = double(piece, "core", 0)
    zs = lax.axis_size("zh") * lax.axis_size("zl")
    xs, cs = lax.axis_size("x"), lax.axis_size("core")
    blocks_in = piece.reshape(cs, xs, zs, -1, piece.shape[1])
    piece = blocks_in.transpose(2, 1, 0, 3, 4).reshape(piece.shape)
    low = jnp.dot(own_context, piece[:, :rank_width], preferred_element_type=jnp.float32).astype(jnp.bfloat16)
    back = jnp.dot(own_cotangent, piece[:, rank_width:], preferred_element_type=jnp.float32).astype(jnp.bfloat16)
    down_part = lax.dot_general(
        own_context, back, (((0,), (0,)), ((), ())), preferred_element_type=jnp.float32
    )
    up_part = lax.dot_general(
        own_cotangent, low, (((0,), (0,)), ((), ())), preferred_element_type=jnp.float32
    )
    grad_rows = jnp.concatenate([down_part, up_part], axis=1)
    full = grad_rows.shape
    by_core = grad_rows.reshape(zs * xs, cs, -1, full[1])
    me = lax.axis_index("core")
    mine = lax.dynamic_index_in_dim(by_core, me, 1, keepdims=False).reshape(-1, full[1])
    other = lax.dynamic_index_in_dim(by_core, 1 - me, 1, keepdims=False).reshape(-1, full[1])
    grad_rows = mine + lax.ppermute(other, "core", [(0, 1), (1, 0)])
    grad_rows = lax.psum_scatter(grad_rows, Z, scatter_dimension=0, tiled=True)
    tasks = lax.axis_size("task")
    rows, width = grad_rows.shape
    tiles = grad_rows.reshape(xs, rows // xs, tasks, width // tasks).transpose(0, 2, 1, 3)
    tiles = tiles.reshape(xs * tasks, rows // xs, width // tasks)
    tiles = lax.all_to_all(tiles, ("x", "task"), 0, 0, tiled=True)
    tiles = tiles.reshape(xs, tasks, rows // xs, width // tasks)
    pieces = tiles[0]
    for position in range(1, xs):
        pieces = pieces + tiles[position]
    partial_gram = jnp.einsum("sij,tij->st", pieces, pieces, precision=lax.Precision.HIGHEST)
    gram_matrix = butterfly_sum(partial_gram, "core")
    for axis in ("x", "zl", "zh", "task"):
        gathered = gather_rows(gram_matrix, axis)
        gram_matrix = gathered[0]
        for position in range(1, gathered.shape[0]):
            gram_matrix = gram_matrix + gathered[position]
    return tail(gram_matrix, pieces, moment_one, moment_two)


def solution(mesh):
    tasks, fsdp = mesh.devices.shape
    split = Mesh(mesh.devices.reshape(tasks, fsdp // 32, 4, 4, 2), ("task",) + FSDP)
    in_specs = (
        P("task", FSDP, None),
        P("task", FSDP, None),
        P(FSDP, None),
        P(FSDP, "task"),
        P(FSDP, "task"),
    )
    out_specs = (P(FSDP, "task"), P(FSDP, "task"), P(FSDP, "task"))
    return jax.shard_map(body, mesh=split, in_specs=in_specs, out_specs=out_specs, check_vma=False)
```

```python
import math

import jax
import jax.numpy as jnp
from jax import lax
from jax.experimental import pallas as pl
from jax.sharding import Mesh
from jax.sharding import PartitionSpec as P

D = 4096
RANK = 128
FSDP = ("z", "x", "core")
ALL_AXES = ("core", "x", "z", "task")


def tail_kernel(gram_ref, gramt_ref, pieces_ref, m1_ref, m2_ref, first_ref, second_ref, step_ref):
    gram = gram_ref[...]
    kt = gramt_ref[...]
    shape = gram.shape
    row = lax.broadcasted_iota(jnp.int32, shape, 0)
    lane = lax.broadcasted_iota(jnp.int32, shape, 1)

    def lanes(x):
        return jnp.sum(x, axis=1, keepdims=True)

    def sublanes(x):
        return jnp.sum(x, axis=0, keepdims=True)

    def pick(x, r, l):
        return lanes(sublanes(jnp.where((row == r) & (lane == l), x, 0.0)))

    norm_col = jnp.sqrt(lanes(jnp.where(row == lane, gram, 0.0)))
    k00 = pick(gram, 0, 0)
    n0 = jnp.sqrt(k00)
    k_i0 = sublanes(jnp.where(row == 0, kt, 0.0))
    k_0j = lanes(jnp.where(lane == 0, kt, 0.0))
    system = (k00 - k_i0) / n0 - (k_0j - kt) / norm_col
    right = k00 / n0 - k_0j / norm_col
    aug = jnp.where(lane == 0, right, system)
    tasks = pieces_ref.shape[0]
    for column in range(1, tasks):
        pivot_row = sublanes(jnp.where(row == column, aug, 0.0))
        column_vals = lanes(jnp.where(lane == column, aug, 0.0))
        pivot = lanes(jnp.where(lane[:1] == column, pivot_row, 0.0))
        factor = column_vals / pivot
        aug = jnp.where(row > column, aug - factor * pivot_row, aug)
    answer = [None] * tasks
    lane_row = lax.broadcasted_iota(jnp.int32, (1, shape[1]), 1)
    row_col = lax.broadcasted_iota(jnp.int32, (shape[0], 1), 0)
    for column in reversed(range(1, tasks)):
        pivot_row = sublanes(jnp.where(row == column, aug, 0.0))
        running = lanes(jnp.where(lane_row == 0, pivot_row, 0.0))
        for follow in range(column + 1, tasks):
            running = running - lanes(jnp.where(lane_row == follow, pivot_row, 0.0)) * answer[follow]
        answer[column] = running / lanes(jnp.where(lane_row == column, pivot_row, 0.0))
    total = answer[1]
    for column in range(2, tasks):
        total = total + answer[column]
    answer[0] = 1.0 - total
    alpha_row = jnp.zeros((1, shape[1]), jnp.float32)
    alpha_col = jnp.zeros((shape[0], 1), jnp.float32)
    for t in range(tasks):
        alpha_row = jnp.where(lane_row == t, answer[t], alpha_row)
        alpha_col = jnp.where(row_col == t, answer[t], alpha_col)
    combined = answer[0] * pieces_ref[0]
    for t in range(1, tasks):
        combined = combined + answer[t] * pieces_ref[t]
    squared = sublanes(alpha_col * lanes(gram * alpha_row))
    grad_norm = jnp.sqrt(1e-06 + squared)
    clipped = combined * (math.sqrt(2 * RANK * D) / grad_norm)
    first = 0.9 * m1_ref[...] + 0.1 * clipped
    second = 0.95 * m2_ref[...] + 0.05 * clipped * clipped
    first_ref[...] = first
    second_ref[...] = second
    step_ref[...] = first / (1.0 - 0.9**20) / (jnp.sqrt(second / (1.0 - 0.95**20)) + 1e-08)


def tail(gram, pieces, moment_one, moment_two):
    tasks = gram.shape[0]
    padded = jnp.zeros((8, 128), jnp.float32).at[:tasks, :tasks].set(gram)
    padded_t = jnp.zeros((8, 128), jnp.float32).at[:tasks, :tasks].set(gram.T)
    out = jax.ShapeDtypeStruct(moment_one.shape, jnp.float32)
    return pl.pallas_call(tail_kernel, out_shape=(out, out, out))(
        padded, padded_t, pieces, moment_one, moment_two
    )


def halve(value, axis, bit):
    me = (lax.axis_index(axis) >> bit) & 1
    size = lax.axis_size(axis)
    halves = value.reshape((2, value.shape[0] // 2) + value.shape[1:])
    mine = lax.dynamic_index_in_dim(halves, me, 0, keepdims=False)
    other = lax.dynamic_index_in_dim(halves, 1 - me, 0, keepdims=False)
    pairs = [(i, i ^ (1 << bit)) for i in range(size)]
    return mine + lax.ppermute(other, axis, pairs)


def double(value, axis, bit):
    me = (lax.axis_index(axis) >> bit) & 1
    size = lax.axis_size(axis)
    pairs = [(i, i ^ (1 << bit)) for i in range(size)]
    other = lax.ppermute(value, axis, pairs)
    first = jnp.where(me == 0, value, other)
    second = jnp.where(me == 0, other, value)
    return jnp.concatenate([first, second], axis=0)


def gather_rows(value, axis):
    size = lax.axis_size(axis)
    copies = jnp.broadcast_to(value[None], (size,) + value.shape)
    return lax.all_to_all(copies, axis, 0, 0, tiled=True)


def butterfly_sum(value, axis):
    size = lax.axis_size(axis)
    step = 1
    while step < size:
        pairs = [(i, i ^ step) for i in range(size)]
        value = value + lax.ppermute(value, axis, pairs)
        step *= 2
    return value


def body(contexts, cotangents, adapter, moment_one, moment_two):
    own_context = contexts[0]
    own_cotangent = cotangents[0]
    rank_width = adapter.shape[1] // 2
    piece = gather_rows(adapter, "z")
    piece = gather_rows(piece, "x").reshape(-1, adapter.shape[1])
    piece = double(piece, "core", 0)
    zs, xs, cs = (lax.axis_size(a) for a in FSDP)
    blocks_in = piece.reshape(cs, xs, zs, -1, piece.shape[1])
    piece = blocks_in.transpose(2, 1, 0, 3, 4).reshape(piece.shape)
    low = jnp.dot(own_context, piece[:, :rank_width], preferred_element_type=jnp.float32).astype(jnp.bfloat16)
    back = jnp.dot(own_cotangent, piece[:, rank_width:], preferred_element_type=jnp.float32).astype(jnp.bfloat16)
    down_part = lax.dot_general(
        own_context, back, (((0,), (0,)), ((), ())), preferred_element_type=jnp.float32
    )
    up_part = lax.dot_general(
        own_cotangent, low, (((0,), (0,)), ((), ())), preferred_element_type=jnp.float32
    )
    me = lax.axis_index("core")

    def core_half(index):
        parts = [
            lax.dynamic_index_in_dim(part.reshape(zs * xs, cs, -1, part.shape[1]), index, 1, keepdims=False)
            for part in (down_part, up_part)
        ]
        joined = jnp.concatenate(parts, axis=-1)
        return joined.reshape(-1, joined.shape[-1])

    mine = core_half(me)
    other = core_half(1 - me)
    grad_rows = mine + lax.ppermute(other, "core", [(0, 1), (1, 0)])
    grad_rows = lax.psum_scatter(grad_rows, "z", scatter_dimension=0, tiled=True)
    tasks = lax.axis_size("task")
    rows, width = grad_rows.shape
    tiles = grad_rows.reshape(xs, rows // xs, tasks, width // tasks).transpose(0, 2, 1, 3)
    tiles = tiles.reshape(xs * tasks, rows // xs, width // tasks)
    tiles = lax.all_to_all(tiles, ("x", "task"), 0, 0, tiled=True)
    tiles = tiles.reshape(xs, tasks, rows // xs, width // tasks)
    pieces = tiles[0]
    for position in range(1, xs):
        pieces = pieces + tiles[position]
    partial_gram = jnp.einsum("sij,tij->st", pieces, pieces, precision=lax.Precision.HIGHEST)
    gram_matrix = butterfly_sum(partial_gram, "core")
    for axis in ("x", "z", "task"):
        gathered = gather_rows(gram_matrix, axis)
        gram_matrix = gathered[0]
        for position in range(1, gathered.shape[0]):
            gram_matrix = gram_matrix + gathered[position]
    return tail(gram_matrix, pieces, moment_one, moment_two)


def solution(mesh):
    tasks, fsdp = mesh.devices.shape
    split = Mesh(mesh.devices.reshape(tasks, fsdp // 8, 4, 2), ("task",) + FSDP)
    in_specs = (
        P("task", FSDP, None),
        P("task", FSDP, None),
        P(FSDP, None),
        P(FSDP, "task"),
        P(FSDP, "task"),
    )
    out_specs = (P(FSDP, "task"), P(FSDP, "task"), P(FSDP, "task"))
    return jax.shard_map(body, mesh=split, in_specs=in_specs, out_specs=out_specs, check_vma=False)
```

```python
import math

import jax
import jax.numpy as jnp
from jax import lax
from jax.experimental import pallas as pl
from jax.sharding import Mesh
from jax.sharding import PartitionSpec as P

D = 4096
RANK = 128
FSDP = ("z", "x", "core")
ALL_AXES = ("core", "x", "z", "task")


def tail_kernel(gram_ref, gramt_ref, pieces_ref, m1_ref, m2_ref, first_ref, second_ref, step_ref):
    gram = gram_ref[...]
    kt = gramt_ref[...]
    shape = gram.shape
    row = lax.broadcasted_iota(jnp.int32, shape, 0)
    lane = lax.broadcasted_iota(jnp.int32, shape, 1)

    def lanes(x):
        return jnp.sum(x, axis=1, keepdims=True)

    def sublanes(x):
        return jnp.sum(x, axis=0, keepdims=True)

    def pick(x, r, l):
        return lanes(sublanes(jnp.where((row == r) & (lane == l), x, 0.0)))

    norm_col = jnp.sqrt(lanes(jnp.where(row == lane, gram, 0.0)))
    k00 = pick(gram, 0, 0)
    n0 = jnp.sqrt(k00)
    k_i0 = sublanes(jnp.where(row == 0, kt, 0.0))
    k_0j = lanes(jnp.where(lane == 0, kt, 0.0))
    system = (k00 - k_i0) / n0 - (k_0j - kt) / norm_col
    right = k00 / n0 - k_0j / norm_col
    aug = jnp.where(lane == 0, right, system)
    tasks = pieces_ref.shape[0]
    for column in range(1, tasks):
        pivot_row = sublanes(jnp.where(row == column, aug, 0.0))
        column_vals = lanes(jnp.where(lane == column, aug, 0.0))
        pivot = lanes(jnp.where(lane[:1] == column, pivot_row, 0.0))
        factor = column_vals / pivot
        aug = jnp.where(row > column, aug - factor * pivot_row, aug)
    answer = [None] * tasks
    lane_row = lax.broadcasted_iota(jnp.int32, (1, shape[1]), 1)
    row_col = lax.broadcasted_iota(jnp.int32, (shape[0], 1), 0)
    for column in reversed(range(1, tasks)):
        pivot_row = sublanes(jnp.where(row == column, aug, 0.0))
        running = lanes(jnp.where(lane_row == 0, pivot_row, 0.0))
        for follow in range(column + 1, tasks):
            running = running - lanes(jnp.where(lane_row == follow, pivot_row, 0.0)) * answer[follow]
        answer[column] = running / lanes(jnp.where(lane_row == column, pivot_row, 0.0))
    total = answer[1]
    for column in range(2, tasks):
        total = total + answer[column]
    answer[0] = 1.0 - total
    alpha_row = jnp.zeros((1, shape[1]), jnp.float32)
    alpha_col = jnp.zeros((shape[0], 1), jnp.float32)
    for t in range(tasks):
        alpha_row = jnp.where(lane_row == t, answer[t], alpha_row)
        alpha_col = jnp.where(row_col == t, answer[t], alpha_col)
    combined = answer[0] * pieces_ref[0]
    for t in range(1, tasks):
        combined = combined + answer[t] * pieces_ref[t]
    squared = sublanes(alpha_col * lanes(gram * alpha_row))
    grad_norm = jnp.sqrt(1e-06 + squared)
    clipped = combined * (math.sqrt(2 * RANK * D) / grad_norm)
    first = 0.9 * m1_ref[...] + 0.1 * clipped
    second = 0.95 * m2_ref[...] + 0.05 * clipped * clipped
    first_ref[...] = first
    second_ref[...] = second
    step_ref[...] = first / (1.0 - 0.9**20) / (jnp.sqrt(second / (1.0 - 0.95**20)) + 1e-08)


def tail(gram, pieces, moment_one, moment_two):
    tasks = gram.shape[0]
    padded = jnp.zeros((8, 128), jnp.float32).at[:tasks, :tasks].set(gram)
    padded_t = jnp.zeros((8, 128), jnp.float32).at[:tasks, :tasks].set(gram.T)
    out = jax.ShapeDtypeStruct(moment_one.shape, jnp.float32)
    return pl.pallas_call(tail_kernel, out_shape=(out, out, out))(
        padded, padded_t, pieces, moment_one, moment_two
    )


def halve(value, axis, bit):
    me = (lax.axis_index(axis) >> bit) & 1
    size = lax.axis_size(axis)
    halves = value.reshape((2, value.shape[0] // 2) + value.shape[1:])
    mine = lax.dynamic_index_in_dim(halves, me, 0, keepdims=False)
    other = lax.dynamic_index_in_dim(halves, 1 - me, 0, keepdims=False)
    pairs = [(i, i ^ (1 << bit)) for i in range(size)]
    return mine + lax.ppermute(other, axis, pairs)


def double(value, axis, bit):
    me = (lax.axis_index(axis) >> bit) & 1
    size = lax.axis_size(axis)
    pairs = [(i, i ^ (1 << bit)) for i in range(size)]
    other = lax.ppermute(value, axis, pairs)
    first = jnp.where(me == 0, value, other)
    second = jnp.where(me == 0, other, value)
    return jnp.concatenate([first, second], axis=0)


def gather_rows(value, axis):
    names = axis if isinstance(axis, tuple) else (axis,)
    size = math.prod(lax.axis_size(name) for name in names)
    copies = jnp.broadcast_to(value[None], (size,) + value.shape)
    return lax.all_to_all(copies, axis, 0, 0, tiled=True)


def butterfly_sum(value, axis):
    size = lax.axis_size(axis)
    step = 1
    while step < size:
        pairs = [(i, i ^ step) for i in range(size)]
        value = value + lax.ppermute(value, axis, pairs)
        step *= 2
    return value


def body(contexts, cotangents, adapter, moment_one, moment_two):
    own_context = contexts[0]
    own_cotangent = cotangents[0]
    rank_width = adapter.shape[1] // 2
    piece = gather_rows(adapter, "z")
    piece = gather_rows(piece, ("x", "core"))
    zs, xs, cs = (lax.axis_size(a) for a in FSDP)
    blocks_in = piece.reshape((xs, cs, zs) + adapter.shape)
    piece = blocks_in.transpose(2, 0, 1, 3, 4).reshape(-1, adapter.shape[1])
    low = jnp.dot(own_context, piece[:, :rank_width], preferred_element_type=jnp.float32).astype(jnp.bfloat16)
    back = jnp.dot(own_cotangent, piece[:, rank_width:], preferred_element_type=jnp.float32).astype(jnp.bfloat16)
    down_part = lax.dot_general(
        own_context, back, (((0,), (0,)), ((), ())), preferred_element_type=jnp.float32
    )
    up_part = lax.dot_general(
        own_cotangent, low, (((0,), (0,)), ((), ())), preferred_element_type=jnp.float32
    )
    me = lax.axis_index("core")

    def core_half(index):
        parts = [
            lax.dynamic_index_in_dim(part.reshape(zs * xs, cs, -1, part.shape[1]), index, 1, keepdims=False)
            for part in (down_part, up_part)
        ]
        joined = jnp.concatenate(parts, axis=-1)
        return joined.reshape(-1, joined.shape[-1])

    mine = core_half(me)
    other = core_half(1 - me)
    grad_rows = mine + lax.ppermute(other, "core", [(0, 1), (1, 0)])
    grad_rows = lax.psum_scatter(grad_rows, "z", scatter_dimension=0, tiled=True)
    tasks = lax.axis_size("task")
    rows, width = grad_rows.shape
    tiles = grad_rows.reshape(xs, rows // xs, tasks, width // tasks).transpose(0, 2, 1, 3)
    tiles = tiles.reshape(xs * tasks, rows // xs, width // tasks)
    tiles = lax.all_to_all(tiles, ("x", "task"), 0, 0, tiled=True)
    tiles = tiles.reshape(xs, tasks, rows // xs, width // tasks)
    pieces = tiles[0]
    for position in range(1, xs):
        pieces = pieces + tiles[position]
    partial_gram = jnp.einsum("sij,tij->st", pieces, pieces, precision=lax.Precision.HIGHEST)
    gram_matrix = partial_gram
    for axis in (("x", "core"), "z", "task"):
        gathered = gather_rows(gram_matrix, axis)
        gram_matrix = gathered[0]
        for position in range(1, gathered.shape[0]):
            gram_matrix = gram_matrix + gathered[position]
    return tail(gram_matrix, pieces, moment_one, moment_two)


def solution(mesh):
    tasks, fsdp = mesh.devices.shape
    split = Mesh(mesh.devices.reshape(tasks, fsdp // 8, 4, 2), ("task",) + FSDP)
    in_specs = (
        P("task", FSDP, None),
        P("task", FSDP, None),
        P(FSDP, None),
        P(FSDP, "task"),
        P(FSDP, "task"),
    )
    out_specs = (P(FSDP, "task"), P(FSDP, "task"), P(FSDP, "task"))
    return jax.shard_map(body, mesh=split, in_specs=in_specs, out_specs=out_specs, check_vma=False)
```

```python
import math

import jax
import jax.numpy as jnp
from jax import lax
from jax.experimental import pallas as pl
from jax.sharding import Mesh
from jax.sharding import PartitionSpec as P

D = 4096
RANK = 128
FSDP = ("z", "x", "core")
ALL_AXES = ("core", "x", "z", "task")


def tail_kernel(gram_ref, gramt_ref, pieces_ref, m1_ref, m2_ref, first_ref, second_ref, step_ref):
    gram = gram_ref[...]
    kt = gramt_ref[...]
    shape = gram.shape
    row = lax.broadcasted_iota(jnp.int32, shape, 0)
    lane = lax.broadcasted_iota(jnp.int32, shape, 1)

    def lanes(x):
        return jnp.sum(x, axis=1, keepdims=True)

    def sublanes(x):
        return jnp.sum(x, axis=0, keepdims=True)

    def pick(x, r, l):
        return lanes(sublanes(jnp.where((row == r) & (lane == l), x, 0.0)))

    norm_col = jnp.sqrt(lanes(jnp.where(row == lane, gram, 0.0)))
    k00 = pick(gram, 0, 0)
    n0 = jnp.sqrt(k00)
    k_i0 = sublanes(jnp.where(row == 0, kt, 0.0))
    k_0j = lanes(jnp.where(lane == 0, kt, 0.0))
    system = (k00 - k_i0) / n0 - (k_0j - kt) / norm_col
    right = k00 / n0 - k_0j / norm_col
    aug = jnp.where(lane == 0, right, system)
    tasks = pieces_ref.shape[0]
    for column in range(1, tasks):
        pivot_row = sublanes(jnp.where(row == column, aug, 0.0))
        column_vals = lanes(jnp.where(lane == column, aug, 0.0))
        pivot = lanes(jnp.where(lane[:1] == column, pivot_row, 0.0))
        factor = column_vals / pivot
        aug = jnp.where(row > column, aug - factor * pivot_row, aug)
    answer = [None] * tasks
    lane_row = lax.broadcasted_iota(jnp.int32, (1, shape[1]), 1)
    row_col = lax.broadcasted_iota(jnp.int32, (shape[0], 1), 0)
    for column in reversed(range(1, tasks)):
        pivot_row = sublanes(jnp.where(row == column, aug, 0.0))
        running = lanes(jnp.where(lane_row == 0, pivot_row, 0.0))
        for follow in range(column + 1, tasks):
            running = running - lanes(jnp.where(lane_row == follow, pivot_row, 0.0)) * answer[follow]
        answer[column] = running / lanes(jnp.where(lane_row == column, pivot_row, 0.0))
    total = answer[1]
    for column in range(2, tasks):
        total = total + answer[column]
    answer[0] = 1.0 - total
    alpha_row = jnp.zeros((1, shape[1]), jnp.float32)
    alpha_col = jnp.zeros((shape[0], 1), jnp.float32)
    for t in range(tasks):
        alpha_row = jnp.where(lane_row == t, answer[t], alpha_row)
        alpha_col = jnp.where(row_col == t, answer[t], alpha_col)
    combined = answer[0] * pieces_ref[0]
    for t in range(1, tasks):
        combined = combined + answer[t] * pieces_ref[t]
    squared = sublanes(alpha_col * lanes(gram * alpha_row))
    grad_norm = jnp.sqrt(1e-06 + squared)
    clipped = combined * (math.sqrt(2 * RANK * D) / grad_norm)
    first = 0.9 * m1_ref[...] + 0.1 * clipped
    second = 0.95 * m2_ref[...] + 0.05 * clipped * clipped
    first_ref[...] = first
    second_ref[...] = second
    step_ref[...] = first / (1.0 - 0.9**20) / (jnp.sqrt(second / (1.0 - 0.95**20)) + 1e-08)


def tail(gram, pieces, moment_one, moment_two):
    tasks = gram.shape[0]
    padded = jnp.zeros((8, 128), jnp.float32).at[:tasks, :tasks].set(gram)
    padded_t = jnp.zeros((8, 128), jnp.float32).at[:tasks, :tasks].set(gram.T)
    out = jax.ShapeDtypeStruct(moment_one.shape, jnp.float32)
    return pl.pallas_call(tail_kernel, out_shape=(out, out, out))(
        padded, padded_t, pieces, moment_one, moment_two
    )


def halve(value, axis, bit):
    me = (lax.axis_index(axis) >> bit) & 1
    size = lax.axis_size(axis)
    halves = value.reshape((2, value.shape[0] // 2) + value.shape[1:])
    mine = lax.dynamic_index_in_dim(halves, me, 0, keepdims=False)
    other = lax.dynamic_index_in_dim(halves, 1 - me, 0, keepdims=False)
    pairs = [(i, i ^ (1 << bit)) for i in range(size)]
    return mine + lax.ppermute(other, axis, pairs)


def double(value, axis, bit):
    me = (lax.axis_index(axis) >> bit) & 1
    size = lax.axis_size(axis)
    pairs = [(i, i ^ (1 << bit)) for i in range(size)]
    other = lax.ppermute(value, axis, pairs)
    first = jnp.where(me == 0, value, other)
    second = jnp.where(me == 0, other, value)
    return jnp.concatenate([first, second], axis=0)


def gather_rows(value, axis):
    names = axis if isinstance(axis, tuple) else (axis,)
    size = math.prod(lax.axis_size(name) for name in names)
    copies = jnp.broadcast_to(value[None], (size,) + value.shape)
    return lax.all_to_all(copies, axis, 0, 0, tiled=True)


def butterfly_sum(value, axis):
    size = lax.axis_size(axis)
    step = 1
    while step < size:
        pairs = [(i, i ^ step) for i in range(size)]
        value = value + lax.ppermute(value, axis, pairs)
        step *= 2
    return value


def body(contexts, cotangents, adapter, moment_one, moment_two):
    own_context = contexts[0]
    own_cotangent = cotangents[0]
    rank_width = adapter.shape[1] // 2
    piece = gather_rows(adapter, "z")
    piece = gather_rows(piece, "x").reshape(-1, adapter.shape[1])
    piece = double(piece, "core", 0)
    zs, xs, cs = (lax.axis_size(a) for a in FSDP)
    blocks_in = piece.reshape(cs, xs, zs, -1, piece.shape[1])
    piece = blocks_in.transpose(2, 1, 0, 3, 4).reshape(piece.shape)
    low = jnp.dot(own_context, piece[:, :rank_width], preferred_element_type=jnp.float32).astype(jnp.bfloat16)
    back = jnp.dot(own_cotangent, piece[:, rank_width:], preferred_element_type=jnp.float32).astype(jnp.bfloat16)
    down_part = lax.dot_general(
        own_context, back, (((0,), (0,)), ((), ())), preferred_element_type=jnp.float32
    )
    up_part = lax.dot_general(
        own_cotangent, low, (((0,), (0,)), ((), ())), preferred_element_type=jnp.float32
    )
    me = lax.axis_index("core")

    def core_half(index):
        parts = [
            lax.dynamic_index_in_dim(part.reshape(zs * xs, cs, -1, part.shape[1]), index, 1, keepdims=False)
            for part in (down_part, up_part)
        ]
        joined = jnp.concatenate(parts, axis=-1)
        return joined.reshape(-1, joined.shape[-1])

    mine = core_half(me)
    other = core_half(1 - me)
    grad_rows = mine + lax.ppermute(other, "core", [(0, 1), (1, 0)])
    grad_rows = lax.psum_scatter(grad_rows, "z", scatter_dimension=0, tiled=True)
    tasks = lax.axis_size("task")
    rows, width = grad_rows.shape
    tiles = grad_rows.reshape(xs, rows // xs, tasks, width // tasks).transpose(0, 2, 1, 3)
    tiles = tiles.reshape(xs * tasks, rows // xs, width // tasks)
    tiles = lax.all_to_all(tiles, ("x", "task"), 0, 0, tiled=True)
    tiles = tiles.reshape(xs, tasks, rows // xs, width // tasks)
    pieces = tiles[0]
    for position in range(1, xs):
        pieces = pieces + tiles[position]
    partial_gram = jnp.einsum("sij,tij->st", pieces, pieces, precision=lax.Precision.HIGHEST)
    gram_matrix = partial_gram
    for axis in (("x", "core"), "z", "task"):
        gathered = gather_rows(gram_matrix, axis)
        gram_matrix = gathered[0]
        for position in range(1, gathered.shape[0]):
            gram_matrix = gram_matrix + gathered[position]
    return tail(gram_matrix, pieces, moment_one, moment_two)


def solution(mesh):
    tasks, fsdp = mesh.devices.shape
    split = Mesh(mesh.devices.reshape(tasks, fsdp // 8, 4, 2), ("task",) + FSDP)
    in_specs = (
        P("task", FSDP, None),
        P("task", FSDP, None),
        P(FSDP, None),
        P(FSDP, "task"),
        P(FSDP, "task"),
    )
    out_specs = (P(FSDP, "task"), P(FSDP, "task"), P(FSDP, "task"))
    return jax.shard_map(body, mesh=split, in_specs=in_specs, out_specs=out_specs, check_vma=False)
```
